256 devices in a mesh: row: 8 (over x, core), col: 32 (over y, z).
Axes of the slice: x: 4, y: 4, z: 8, core: 2. Of those that a mesh axis runs over, the one named last changes fastest.
Arguments:
- tokens: bfloat16 [1024, 6144], P('col', 'row'), may hold values from -6 to 6
- w_up: bfloat16 [6144, 24576], P('row', 'col'), may hold values from -0.078125 to 0.078125
- w_down: bfloat16 [24576, 6144], P('col', 'row'), may hold values from -0.0390625 to 0.0390625
- expert_in: bfloat16 [6144, 8192], P(None, 'col'), may hold values from -0.078125 to 0.078125
- expert_out: bfloat16 [8192, 6144], P('col'), may hold values from -0.125 to 0.125
- expert_ids: int32 [1024, 2], P('col'), may hold values from 0 to 3, as said below
- route_weights: bfloat16 [1024, 2], P('col'), may hold values from 0.25 to 1
- out_grad: bfloat16 [1024, 6144], P('col', 'row'), may hold values from -6 to 6
Outputs:
- layer_out: bfloat16 [1024, 6144], P('col', 'row')
- tokens_grad: bfloat16 [1024, 6144], P('col', 'row')
- up_grad: bfloat16 [6144, 24576], P('row', 'col')
- down_grad: bfloat16 [24576, 6144], P('col', 'row')
- expert_in_grad: bfloat16 [6144, 8192], P('row', 'col')
- expert_out_grad: bfloat16 [8192, 6144], P('col', 'row')
The draws below stay inside these ranges and needn't reach their ends.
Inputs may be any that keep to these rules, and one draw needn't show every extreme that they name: `expert_ids`: the two experts of a token differ. In every aligned block of 4 tokens no expert is named by more than 3 of the block's pairs; one expert is named by exactly 3 pairs, the same expert in all blocks whose index leaves the same remainder modulo 32 // 4; the other experts' counts in a block differ by at most one. Every expert is named somewhere.
All inputs are finite; a program needn't handle non-finite values.
Results may differ from the reference program's by a relative error of at most 0.025.
Values may be sent and summed in bfloat16 or wider, within the bound.
No kernel may reach another device: no remote copies, remote signals or barrier semaphores. Data moves between devices by JAX's collectives and lax.ppermute only.
A program may use at most 128 MiB of HBM per device.

```python
import jax
import jax.numpy as jnp
from jax import lax

D = 6144
FF = 24576
EXPERTS = 4
EH = 2048
TOK_COL = 32
TOKENS = 1024
BLOCK = 4
CAP = 3
N_ROW = 8
N_COL = 32


def route_tables(key):
    base = jax.random.fold_in(key, 11)
    key_lead, key_order, key_shift = jax.random.split(base, 3)
    block_count = TOKENS // BLOCK
    group_count = TOK_COL // BLOCK
    leaders = jax.random.randint(key_lead, (group_count,), 0, EXPERTS)
    block_lead = leaders[jnp.arange(block_count) % group_count][:, None]
    orders = jax.vmap(lambda sub: jax.random.permutation(sub, BLOCK))(jax.random.split(key_order, block_count))
    places = jnp.argsort(orders, axis=1).astype(jnp.int32)
    shifts = jax.random.randint(key_shift, (block_count, 1), 0, EXPERTS - 1)
    others = EXPERTS - 1
    leading = places < CAP
    sequence = jnp.where(leading, places, CAP + 2 * (places - CAP))

    def other_expert(rank):
        return rank + (rank >= block_lead).astype(jnp.int32)
    first_pick = jnp.where(leading, block_lead, other_expert((shifts + sequence) % others))
    second_pick = jnp.where(leading, other_expert((shifts + sequence) % others), other_expert((shifts + sequence + 1) % others))
    chosen = jnp.stack([first_pick, second_pick], axis=-1).astype(jnp.int32)
    return chosen.reshape(TOKENS, 2)


def draw_expert_ids(key, part):
    return route_tables(key)


def block_scale(key, dims, shards, low, largest):
    gain = 1.0
    for dim, blocks in shards:
        draws = jax.random.uniform(jax.random.fold_in(jax.random.fold_in(key, 6), dim), (blocks,), jnp.float32, low / len(shards), largest / len(shards))
        gain = gain * jnp.repeat(jnp.exp(draws), dims[dim] // blocks).reshape((-1,) + (1,) * (len(dims) - 1 - dim))
    return gain


def gaussian(stream_key, shape, spread, most, cuts=(), held_as=jnp.bfloat16):
    array = spread * jax.random.normal(stream_key, shape, jnp.float32)
    if cuts:
        array = array * block_scale(stream_key, shape, cuts, -0.22, 0.18)
    return jnp.clip(array, -most, most).astype(held_as)


def setup_inputs(seed: int = 0) -> dict:
    splits = jax.random.split(jax.random.key(seed), 9)
    return {
        "tokens": gaussian(splits[0], (TOKENS, D), 1.0, 6.0, ((0, 32), (1, 8))),
        "w_up": gaussian(splits[1], (D, FF), D ** -0.5, 0.078125, ((0, 8), (1, 32))),
        "w_down": gaussian(splits[2], (FF, D), FF ** -0.5, 0.0390625, ((0, 32), (1, 8))),
        "expert_in": gaussian(splits[3], (D, EXPERTS * EH), D ** -0.5, 0.078125, ((1, 32),)),
        "expert_out": gaussian(splits[4], (EXPERTS * EH, D), EH ** -0.5, 0.125, ((0, 32),)),
        "expert_ids": draw_expert_ids(jax.random.fold_in(splits[8], 71), 0),
        "route_weights": jnp.clip(0.25 + 0.75 * jax.random.uniform(splits[6], (TOKENS, 2), jnp.float32) ** block_scale(splits[6], (TOKENS, 2), ((0, 32),), -0.2, 0.2), 0.25, 1.0).astype(jnp.bfloat16),
        "out_grad": gaussian(splits[7], (TOKENS, D), 1.0, 6.0, ((0, 32), (1, 8))),
    }


gelu_scale = 0.7978845608028654
gelu_cubic = 0.044715


def gelu_tanh(value):
    return 0.5 * value * (1.0 + jnp.tanh(gelu_scale * (value + gelu_cubic * value * value * value)))


def gelu_slope(value):
    inner = jnp.tanh(gelu_scale * (value + gelu_cubic * value * value * value))
    return 0.5 * (1.0 + inner) + 0.5 * value * (1.0 - inner * inner) * gelu_scale * (1.0 + 3.0 * gelu_cubic * value * value)


def rounded(value):
    return lax.optimization_barrier(value.astype(jnp.bfloat16)).astype(jnp.float32)


def block_sum(left, right, blocks):
    stride = left.shape[1] // blocks

    def step(running, position):
        pieces = lax.dynamic_slice_in_dim(left, position * stride, stride, 1)
        panels = lax.dynamic_slice_in_dim(right, position * stride, stride, 0)
        return running + rounded(jnp.dot(pieces, panels, preferred_element_type=jnp.float32)), None

    start = jnp.zeros((left.shape[0], right.shape[1]), jnp.float32)
    running, _ = lax.scan(step, start, jnp.arange(blocks, dtype=jnp.int32))
    return running


def group_sum(left, right):
    left_four = left.reshape(N_COL, N_ROW, BLOCK, left.shape[1])
    right_four = right.reshape(N_COL, N_ROW, BLOCK, right.shape[1])

    def step(running, position):
        left_rows = lax.dynamic_index_in_dim(left_four, position, 1, keepdims=False).reshape(N_COL * BLOCK, left.shape[1])
        right_rows = lax.dynamic_index_in_dim(right_four, position, 1, keepdims=False).reshape(N_COL * BLOCK, right.shape[1])
        return running + rounded(jnp.dot(left_rows.T, right_rows, preferred_element_type=jnp.float32)), None

    start = jnp.zeros((left.shape[1], right.shape[1]), jnp.float32)
    running, _ = lax.scan(step, start, jnp.arange(N_ROW, dtype=jnp.int32))
    return running


def reference(tokens, w_up, w_down, expert_in, expert_out, expert_ids, route_weights, out_grad):
    preact = block_sum(tokens, w_up, N_ROW)
    hidden = gelu_tanh(preact).astype(jnp.bfloat16)
    mixed = (tokens.astype(jnp.float32) + block_sum(hidden, w_down, N_COL)).astype(jnp.bfloat16)
    cotangent = out_grad.astype(jnp.float32)
    moe_sum = jnp.zeros((TOKENS, D), jnp.float32)
    backflow = jnp.zeros((TOKENS, D), jnp.float32)
    in_grads = []
    out_grads = []
    for expert in range(EXPERTS):
        weighting = jnp.sum(route_weights.astype(jnp.float32) * (expert_ids == expert).astype(jnp.float32), axis=1)
        w_in = expert_in[:, expert * EH:(expert + 1) * EH]
        w_out = expert_out[expert * EH:(expert + 1) * EH, :]
        e_pre = jnp.dot(mixed, w_in, preferred_element_type=jnp.float32)
        e_hidden = gelu_tanh(e_pre).astype(jnp.bfloat16)
        moe_sum = moe_sum + weighting[:, None] * jnp.dot(e_hidden, w_out, preferred_element_type=jnp.float32)
        scaled = (weighting[:, None] * cotangent).astype(jnp.bfloat16)
        e_dpre = (jnp.dot(scaled, w_out.T, preferred_element_type=jnp.float32) * gelu_slope(e_pre)).astype(jnp.bfloat16)
        backflow = backflow + jnp.dot(e_dpre, w_in.T, preferred_element_type=jnp.float32)
        in_grads.append(group_sum(mixed, e_dpre))
        out_grads.append(group_sum(e_hidden, scaled))
    layer_out = (mixed.astype(jnp.float32) + moe_sum).astype(jnp.bfloat16)
    mixed_grad = (cotangent + backflow).astype(jnp.bfloat16)
    hidden_grad = block_sum(mixed_grad, w_down.T, N_ROW)
    dense_dpre = (hidden_grad * gelu_slope(preact)).astype(jnp.bfloat16)
    tokens_grad = (mixed_grad.astype(jnp.float32) + block_sum(dense_dpre, w_up.T, N_COL)).astype(jnp.bfloat16)
    up_grad = jnp.dot(tokens.T, dense_dpre, preferred_element_type=jnp.float32).astype(jnp.bfloat16)
    down_grad = jnp.dot(hidden.T, mixed_grad, preferred_element_type=jnp.float32).astype(jnp.bfloat16)
    expert_in_grad = jnp.concatenate(in_grads, axis=1).astype(jnp.bfloat16)
    expert_out_grad = jnp.concatenate(out_grads, axis=0).astype(jnp.bfloat16)
    return (layer_out, tokens_grad, up_grad, down_grad, expert_in_grad, expert_out_grad)
```

```python
import jax
import jax.numpy as jnp
from jax import lax
from jax.sharding import PartitionSpec as P

EXPERTS = 4


gelu_scale = 0.7978845608028654
gelu_cubic = 0.044715


def gelu_tanh(value):
    return 0.5 * value * (1.0 + jnp.tanh(gelu_scale * (value + gelu_cubic * value * value * value)))


def gelu_slope(value):
    inner = jnp.tanh(gelu_scale * (value + gelu_cubic * value * value * value))
    return 0.5 * (1.0 + inner) + 0.5 * value * (1.0 - inner * inner) * gelu_scale * (
        1.0 + 3.0 * gelu_cubic * value * value
    )


def slot_ranks(pairs):
    count = pairs.shape[-1]
    positions = jnp.arange(count, dtype=jnp.int32)
    earlier = positions[:, None] > positions[None, :]
    matching = pairs[..., :, None] == pairs[..., None, :]
    return jnp.sum((matching & earlier).astype(jnp.int32), axis=-1)


def gather_rows(part, axis_name):
    count = lax.axis_size(axis_name)
    spread = jnp.broadcast_to(part[None], (count,) + part.shape)
    got = lax.all_to_all(spread, axis_name, 0, 0, tiled=True)
    return got.reshape((count * part.shape[0],) + part.shape[1:])


def scatter_sum(terms, axis_name):
    count = lax.axis_size(axis_name)
    blocks = terms.astype(jnp.bfloat16).reshape((count, terms.shape[0] // count) + terms.shape[1:])
    got = lax.all_to_all(blocks, axis_name, 0, 0, tiled=True)
    return got.astype(jnp.float32).sum(axis=0)


def scatter_sum_cols(terms, axis_name):
    count = lax.axis_size(axis_name)
    got = lax.all_to_all(terms.astype(jnp.bfloat16), axis_name, 1, 0, tiled=True)
    return got.reshape((count, terms.shape[0], terms.shape[1] // count)).astype(jnp.float32).sum(axis=0)


def on_device(tokens, w_up, w_down, expert_in, expert_out, expert_ids, route_weights, out_grad):
    row_count = lax.axis_size("row")
    col_count = lax.axis_size("col")
    tok_col = tokens.shape[0]
    block_len = tok_col // row_count
    group_len = col_count // EXPERTS
    slot_cap = max(2, 3 * block_len // 4)
    model_width = expert_out.shape[1]
    my_row = lax.axis_index("row")
    tok_panel = gather_rows(tokens, "col")
    up_terms = jnp.dot(tok_panel, w_up, preferred_element_type=jnp.float32)
    preact = scatter_sum(up_terms, "row")
    hidden_full = gather_rows(gelu_tanh(preact).astype(jnp.bfloat16), "row")
    rows_in = hidden_full
    dense_term = scatter_sum(jnp.dot(rows_in, w_down, preferred_element_type=jnp.float32), "col")
    mixed_act = (tokens.astype(jnp.float32) + dense_term).astype(jnp.bfloat16)
    own_rows, own_grad = (
        lax.all_to_all(mixed_act, "row", split_axis=0, concat_axis=1, tiled=True),
        lax.all_to_all(out_grad, "row", split_axis=0, concat_axis=1, tiled=True),
    )
    chosen = lax.dynamic_slice_in_dim(expert_ids, my_row * block_len, block_len, 0).reshape(-1)
    weights_own = lax.dynamic_slice_in_dim(route_weights, my_row * block_len, block_len, 0)
    weights_flat = weights_own.reshape(-1).astype(jnp.float32)
    rows_x = jnp.repeat(own_rows, 2, axis=0)
    scaled = (weights_flat[:, None] * jnp.repeat(own_grad, 2, axis=0).astype(jnp.float32)).astype(
        jnp.bfloat16
    )
    slot_range = jnp.arange(slot_cap, dtype=jnp.int32)
    placed = slot_ranks(chosen)
    expert_range = jnp.arange(EXPERTS, dtype=jnp.int32)
    onehot = (
        (chosen[None, None, :] == expert_range[:, None, None])
        & (placed[None, None, :] == slot_range[None, :, None])
    ).astype(jnp.bfloat16)
    send_x = jnp.einsum("eca,ad->ecd", onehot, rows_x, preferred_element_type=jnp.float32).astype(
        jnp.bfloat16
    )
    send_g = jnp.einsum("eca,ad->ecd", onehot, scaled, preferred_element_type=jnp.float32).astype(
        jnp.bfloat16
    )
    send_x = jnp.repeat(send_x, group_len, axis=0)
    send_g = jnp.repeat(send_g, group_len, axis=0)
    got_x, got_g = (
        lax.all_to_all(send_x, "col", split_axis=0, concat_axis=0, tiled=True),
        lax.all_to_all(send_g, "col", split_axis=0, concat_axis=0, tiled=True),
    )
    inputs = got_x.reshape(-1, model_width)
    grads = got_g.reshape(-1, model_width)
    e_pre = jnp.dot(inputs, expert_in, preferred_element_type=jnp.float32)
    e_hidden = gelu_tanh(e_pre).astype(jnp.bfloat16)
    values = jnp.dot(e_hidden, expert_out, preferred_element_type=jnp.float32)
    e_dpre = (
        jnp.dot(grads, expert_out.T, preferred_element_type=jnp.float32) * gelu_slope(e_pre)
    ).astype(jnp.bfloat16)
    returns = jnp.dot(e_dpre, expert_in.T, preferred_element_type=jnp.float32)
    grad_in = jnp.dot(inputs.T, e_dpre, preferred_element_type=jnp.float32)
    grad_out = jnp.dot(e_hidden.T, grads, preferred_element_type=jnp.float32)
    values, returns, grad_in, grad_out = (values, returns, grad_in, grad_out)
    back_v, back_d = (
        lax.all_to_all(
            values.reshape(col_count, slot_cap, model_width).astype(jnp.bfloat16),
            "col",
            split_axis=0,
            concat_axis=0,
            tiled=True,
        ).astype(jnp.float32),
        lax.all_to_all(
            returns.reshape(col_count, slot_cap, model_width).astype(jnp.bfloat16),
            "col",
            split_axis=0,
            concat_axis=0,
            tiled=True,
        ).astype(jnp.float32),
    )
    flat_v = (
        back_v.reshape(EXPERTS, group_len, slot_cap, model_width)
        .sum(axis=1)
        .reshape(EXPERTS * slot_cap, model_width)
    )
    flat_d = (
        back_d.reshape(EXPERTS, group_len, slot_cap, model_width)
        .sum(axis=1)
        .reshape(EXPERTS * slot_cap, model_width)
    )
    lookup = chosen * slot_cap + placed
    moe_sum = (
        (weights_flat[:, None] * jnp.take(flat_v, lookup, axis=0))
        .reshape(block_len, 2, model_width)
        .sum(axis=1)
    )
    grad_sum = jnp.take(flat_d, lookup, axis=0).reshape(block_len, 2, model_width).sum(axis=1)
    layer_rows = (own_rows.astype(jnp.float32) + moe_sum).astype(jnp.bfloat16)
    grad_rows = (own_grad.astype(jnp.float32) + grad_sum).astype(jnp.bfloat16)
    layer_out, mixed_grad = (
        lax.all_to_all(layer_rows, "row", split_axis=1, concat_axis=0, tiled=True),
        lax.all_to_all(grad_rows, "row", split_axis=1, concat_axis=0, tiled=True),
    )
    expert_in_grad = scatter_sum(grad_in, "row").astype(jnp.bfloat16)
    expert_out_grad = scatter_sum_cols(grad_out, "row").astype(jnp.bfloat16)
    cot_panel = gather_rows(mixed_grad, "col")
    hgrad_terms = jnp.dot(cot_panel, w_down.T, preferred_element_type=jnp.float32)
    down_grad = jnp.dot(hidden_full.T, cot_panel, preferred_element_type=jnp.float32).astype(
        jnp.bfloat16
    )
    hidden_grad = scatter_sum(hgrad_terms, "row")
    dpre_full = gather_rows((hidden_grad * gelu_slope(preact)).astype(jnp.bfloat16), "row")
    up_grad = jnp.dot(tok_panel.T, dpre_full, preferred_element_type=jnp.float32).astype(
        jnp.bfloat16
    )
    rows_in = dpre_full
    input_term = scatter_sum(jnp.dot(rows_in, w_up.T, preferred_element_type=jnp.float32), "col")
    tokens_grad = (mixed_grad.astype(jnp.float32) + input_term).astype(jnp.bfloat16)
    return (layer_out, tokens_grad, up_grad, down_grad, expert_in_grad, expert_out_grad)


def solution(mesh):
    in_specs = (
        P("col", "row"),
        P("row", "col"),
        P("col", "row"),
        P(None, "col"),
        P("col", None),
        P("col", None),
        P("col", None),
        P("col", "row"),
    )
    out_specs = (
        P("col", "row"),
        P("col", "row"),
        P("row", "col"),
        P("col", "row"),
        P("row", "col"),
        P("col", "row"),
    )
    return jax.shard_map(
        on_device, mesh=mesh, in_specs=in_specs, out_specs=out_specs, check_vma=False
    )
```

```python
import jax
import jax.numpy as jnp
from jax import lax
from jax.sharding import PartitionSpec as P

EXPERTS = 4


gelu_scale = 0.7978845608028654
gelu_cubic = 0.044715


def gelu_tanh(value):
    return 0.5 * value * (1.0 + jnp.tanh(gelu_scale * (value + gelu_cubic * value * value * value)))


def gelu_slope(value):
    inner = jnp.tanh(gelu_scale * (value + gelu_cubic * value * value * value))
    return 0.5 * (1.0 + inner) + 0.5 * value * (1.0 - inner * inner) * gelu_scale * (
        1.0 + 3.0 * gelu_cubic * value * value
    )


def slot_ranks(pairs):
    count = pairs.shape[-1]
    positions = jnp.arange(count, dtype=jnp.int32)
    earlier = positions[:, None] > positions[None, :]
    matching = pairs[..., :, None] == pairs[..., None, :]
    return jnp.sum((matching & earlier).astype(jnp.int32), axis=-1)


def gather_rows(part, axis_name):
    count = lax.axis_size(axis_name)
    spread = jnp.broadcast_to(part[None], (count,) + part.shape)
    got = lax.all_to_all(spread, axis_name, 0, 0, tiled=True)
    return got.reshape((count * part.shape[0],) + part.shape[1:])


def scatter_sum(terms, axis_name):
    count = lax.axis_size(axis_name)
    blocks = terms.astype(jnp.bfloat16).reshape((count, terms.shape[0] // count) + terms.shape[1:])
    got = lax.all_to_all(blocks, axis_name, 0, 0, tiled=True)
    return got.astype(jnp.float32).sum(axis=0)


def scatter_sum_cols(terms, axis_name):
    count = lax.axis_size(axis_name)
    got = lax.all_to_all(terms.astype(jnp.bfloat16), axis_name, 1, 0, tiled=True)
    return got.reshape((count, terms.shape[0], terms.shape[1] // count)).astype(jnp.float32).sum(axis=0)


def on_device(tokens, w_up, w_down, expert_in, expert_out, expert_ids, route_weights, out_grad):
    row_count = lax.axis_size("row")
    col_count = lax.axis_size("col")
    tok_col = tokens.shape[0]
    block_len = tok_col // row_count
    group_len = col_count // EXPERTS
    slot_cap = max(2, 3 * block_len // 4)
    model_width = expert_out.shape[1]
    my_row = lax.axis_index("row")
    tok_panel = gather_rows(tokens, "col")
    up_terms = jnp.dot(tok_panel, w_up, preferred_element_type=jnp.float32)
    preact = scatter_sum(up_terms, "row")
    hidden_full = gather_rows(gelu_tanh(preact).astype(jnp.bfloat16), "row")
    rows_in = hidden_full
    dense_term = scatter_sum(jnp.dot(rows_in, w_down, preferred_element_type=jnp.float32), "col")
    mixed_act = (tokens.astype(jnp.float32) + dense_term).astype(jnp.bfloat16)
    own_both = lax.all_to_all(
        jnp.stack([mixed_act, out_grad], axis=1), "row", split_axis=0, concat_axis=2, tiled=True
    )
    own_rows, own_grad = own_both[:, 0], own_both[:, 1]
    chosen = lax.dynamic_slice_in_dim(expert_ids, my_row * block_len, block_len, 0).reshape(-1)
    weights_own = lax.dynamic_slice_in_dim(route_weights, my_row * block_len, block_len, 0)
    weights_flat = weights_own.reshape(-1).astype(jnp.float32)
    rows_x = jnp.repeat(own_rows, 2, axis=0)
    scaled = (weights_flat[:, None] * jnp.repeat(own_grad, 2, axis=0).astype(jnp.float32)).astype(
        jnp.bfloat16
    )
    slot_range = jnp.arange(slot_cap, dtype=jnp.int32)
    placed = slot_ranks(chosen)
    expert_range = jnp.arange(EXPERTS, dtype=jnp.int32)
    onehot = (
        (chosen[None, None, :] == expert_range[:, None, None])
        & (placed[None, None, :] == slot_range[None, :, None])
    ).astype(jnp.bfloat16)
    send_x = jnp.einsum("eca,ad->ecd", onehot, rows_x, preferred_element_type=jnp.float32).astype(
        jnp.bfloat16
    )
    send_g = jnp.einsum("eca,ad->ecd", onehot, scaled, preferred_element_type=jnp.float32).astype(
        jnp.bfloat16
    )
    send_x = jnp.repeat(send_x, group_len, axis=0)
    send_g = jnp.repeat(send_g, group_len, axis=0)
    got_both = lax.all_to_all(
        jnp.concatenate([send_x, send_g], axis=1), "col", split_axis=0, concat_axis=0, tiled=True
    )
    got_x, got_g = got_both[:, :slot_cap], got_both[:, slot_cap:]
    inputs = got_x.reshape(-1, model_width)
    grads = got_g.reshape(-1, model_width)
    e_pre = jnp.dot(inputs, expert_in, preferred_element_type=jnp.float32)
    e_hidden = gelu_tanh(e_pre).astype(jnp.bfloat16)
    values = jnp.dot(e_hidden, expert_out, preferred_element_type=jnp.float32)
    e_dpre = (
        jnp.dot(grads, expert_out.T, preferred_element_type=jnp.float32) * gelu_slope(e_pre)
    ).astype(jnp.bfloat16)
    returns = jnp.dot(e_dpre, expert_in.T, preferred_element_type=jnp.float32)
    grad_in = jnp.dot(inputs.T, e_dpre, preferred_element_type=jnp.float32)
    grad_out = jnp.dot(e_hidden.T, grads, preferred_element_type=jnp.float32)
    values, returns, grad_in, grad_out = (values, returns, grad_in, grad_out)
    back_both = lax.all_to_all(
        jnp.concatenate(
            [
                values.reshape(col_count, slot_cap, model_width).astype(jnp.bfloat16),
                returns.reshape(col_count, slot_cap, model_width).astype(jnp.bfloat16),
            ],
            axis=1,
        ),
        "col",
        split_axis=0,
        concat_axis=0,
        tiled=True,
    ).astype(jnp.float32)
    back_v, back_d = back_both[:, :slot_cap], back_both[:, slot_cap:]
    flat_v = (
        back_v.reshape(EXPERTS, group_len, slot_cap, model_width)
        .sum(axis=1)
        .reshape(EXPERTS * slot_cap, model_width)
    )
    flat_d = (
        back_d.reshape(EXPERTS, group_len, slot_cap, model_width)
        .sum(axis=1)
        .reshape(EXPERTS * slot_cap, model_width)
    )
    lookup = chosen * slot_cap + placed
    moe_sum = (
        (weights_flat[:, None] * jnp.take(flat_v, lookup, axis=0))
        .reshape(block_len, 2, model_width)
        .sum(axis=1)
    )
    grad_sum = jnp.take(flat_d, lookup, axis=0).reshape(block_len, 2, model_width).sum(axis=1)
    layer_rows = (own_rows.astype(jnp.float32) + moe_sum).astype(jnp.bfloat16)
    grad_rows = (own_grad.astype(jnp.float32) + grad_sum).astype(jnp.bfloat16)
    out_both = lax.all_to_all(
        jnp.stack([layer_rows, grad_rows], axis=1), "row", split_axis=2, concat_axis=0, tiled=True
    )
    layer_out, mixed_grad = out_both[:, 0], out_both[:, 1]
    expert_in_grad = lax.psum_scatter(
        grad_in.astype(jnp.bfloat16).astype(jnp.float32), "row", scatter_dimension=0, tiled=True
    ).astype(jnp.bfloat16)
    expert_out_grad = lax.psum_scatter(
        grad_out.astype(jnp.bfloat16).astype(jnp.float32), "row", scatter_dimension=1, tiled=True
    ).astype(jnp.bfloat16)
    cot_panel = gather_rows(mixed_grad, "col")
    hgrad_terms = jnp.dot(cot_panel, w_down.T, preferred_element_type=jnp.float32)
    down_grad = jnp.dot(hidden_full.T, cot_panel, preferred_element_type=jnp.float32).astype(
        jnp.bfloat16
    )
    hidden_grad = scatter_sum(hgrad_terms, "row")
    dpre_full = gather_rows((hidden_grad * gelu_slope(preact)).astype(jnp.bfloat16), "row")
    up_grad = jnp.dot(tok_panel.T, dpre_full, preferred_element_type=jnp.float32).astype(
        jnp.bfloat16
    )
    rows_in = dpre_full
    input_term = scatter_sum(jnp.dot(rows_in, w_up.T, preferred_element_type=jnp.float32), "col")
    tokens_grad = (mixed_grad.astype(jnp.float32) + input_term).astype(jnp.bfloat16)
    return (layer_out, tokens_grad, up_grad, down_grad, expert_in_grad, expert_out_grad)


def solution(mesh):
    in_specs = (
        P("col", "row"),
        P("row", "col"),
        P("col", "row"),
        P(None, "col"),
        P("col", None),
        P("col", None),
        P("col", None),
        P("col", "row"),
    )
    out_specs = (
        P("col", "row"),
        P("col", "row"),
        P("row", "col"),
        P("col", "row"),
        P("row", "col"),
        P("col", "row"),
    )
    return jax.shard_map(
        on_device, mesh=mesh, in_specs=in_specs, out_specs=out_specs, check_vma=False
    )
```

```python
import jax
import jax.numpy as jnp
from jax import lax
from jax.sharding import PartitionSpec as P

EXPERTS = 4


gelu_scale = 0.7978845608028654
gelu_cubic = 0.044715


def gelu_tanh(value):
    return 0.5 * value * (1.0 + jnp.tanh(gelu_scale * (value + gelu_cubic * value * value * value)))


def gelu_slope(value):
    inner = jnp.tanh(gelu_scale * (value + gelu_cubic * value * value * value))
    return 0.5 * (1.0 + inner) + 0.5 * value * (1.0 - inner * inner) * gelu_scale * (
        1.0 + 3.0 * gelu_cubic * value * value
    )


def slot_ranks(pairs):
    count = pairs.shape[-1]
    positions = jnp.arange(count, dtype=jnp.int32)
    earlier = positions[:, None] > positions[None, :]
    matching = pairs[..., :, None] == pairs[..., None, :]
    return jnp.sum((matching & earlier).astype(jnp.int32), axis=-1)


def gather_rows(part, axis_name):
    count = lax.axis_size(axis_name)
    spread = jnp.broadcast_to(part[None], (count,) + part.shape)
    got = lax.all_to_all(spread, axis_name, 0, 0, tiled=True)
    return got.reshape((count * part.shape[0],) + part.shape[1:])


def scatter_sum(terms, axis_name):
    count = lax.axis_size(axis_name)
    blocks = terms.astype(jnp.bfloat16).reshape((count, terms.shape[0] // count) + terms.shape[1:])
    got = lax.all_to_all(blocks, axis_name, 0, 0, tiled=True)
    return got.astype(jnp.float32).sum(axis=0)


def scatter_sum_cols(terms, axis_name):
    count = lax.axis_size(axis_name)
    got = lax.all_to_all(terms.astype(jnp.bfloat16), axis_name, 1, 0, tiled=True)
    return got.reshape((count, terms.shape[0], terms.shape[1] // count)).astype(jnp.float32).sum(axis=0)


def dense_exchange(payload, axis_name):
    shape = payload.shape
    flat = payload.reshape(shape[0], -1, 128)
    got = lax.all_to_all(flat, axis_name, 0, 0, tiled=True)
    return got.reshape(shape)


def swap_blocks(pair, count):
    arrays, tok, width = pair.shape
    block = tok // count
    parts = pair.reshape(arrays, count, block, width).transpose(1, 0, 2, 3)
    got = lax.all_to_all(parts.reshape(count, arrays * block, width), "row", 0, 0, tiled=True)
    got = got.reshape(count, arrays, block, width).transpose(1, 2, 0, 3)
    return got.reshape(arrays, block, count * width)


def unswap_blocks(pair, count):
    arrays, block, full = pair.shape
    width = full // count
    parts = pair.reshape(arrays, block, count, width).transpose(2, 0, 1, 3)
    got = lax.all_to_all(parts.reshape(count, arrays * block, width), "row", 0, 0, tiled=True)
    got = got.reshape(count, arrays, block, width).transpose(1, 0, 2, 3)
    return got.reshape(arrays, count * block, width)


def on_device(tokens, w_up, w_down, expert_in, expert_out, expert_ids, route_weights, out_grad):
    row_count = lax.axis_size("row")
    col_count = lax.axis_size("col")
    tok_col = tokens.shape[0]
    block_len = tok_col // row_count
    group_len = col_count // EXPERTS
    slot_cap = max(2, 3 * block_len // 4)
    model_width = expert_out.shape[1]
    my_row = lax.axis_index("row")
    tok_panel = gather_rows(tokens, "col")
    up_terms = jnp.dot(tok_panel, w_up, preferred_element_type=jnp.float32)
    preact = scatter_sum(up_terms, "row")
    hidden_full = gather_rows(gelu_tanh(preact).astype(jnp.bfloat16), "row")
    rows_in = hidden_full
    dense_term = scatter_sum(jnp.dot(rows_in, w_down, preferred_element_type=jnp.float32), "col")
    mixed_act = (tokens.astype(jnp.float32) + dense_term).astype(jnp.bfloat16)
    own_both = swap_blocks(jnp.stack([mixed_act, out_grad]), row_count)
    own_rows, own_grad = own_both[0], own_both[1]
    chosen = lax.dynamic_slice_in_dim(expert_ids, my_row * block_len, block_len, 0).reshape(-1)
    weights_own = lax.dynamic_slice_in_dim(route_weights, my_row * block_len, block_len, 0)
    weights_flat = weights_own.reshape(-1).astype(jnp.float32)
    rows_x = jnp.repeat(own_rows, 2, axis=0)
    scaled = (weights_flat[:, None] * jnp.repeat(own_grad, 2, axis=0).astype(jnp.float32)).astype(
        jnp.bfloat16
    )
    slot_range = jnp.arange(slot_cap, dtype=jnp.int32)
    placed = slot_ranks(chosen)
    expert_range = jnp.arange(EXPERTS, dtype=jnp.int32)
    onehot = (
        (chosen[None, None, :] == expert_range[:, None, None])
        & (placed[None, None, :] == slot_range[None, :, None])
    ).astype(jnp.bfloat16)
    send_x = jnp.einsum("eca,ad->ecd", onehot, rows_x, preferred_element_type=jnp.float32).astype(
        jnp.bfloat16
    )
    send_g = jnp.einsum("eca,ad->ecd", onehot, scaled, preferred_element_type=jnp.float32).astype(
        jnp.bfloat16
    )
    send_x = jnp.repeat(send_x, group_len, axis=0)
    send_g = jnp.repeat(send_g, group_len, axis=0)
    got_both = dense_exchange(jnp.concatenate([send_x, send_g], axis=1), "col")
    got_x, got_g = got_both[:, :slot_cap], got_both[:, slot_cap:]
    inputs = got_x.reshape(-1, model_width)
    grads = got_g.reshape(-1, model_width)
    e_pre = jnp.dot(inputs, expert_in, preferred_element_type=jnp.float32)
    e_hidden = gelu_tanh(e_pre).astype(jnp.bfloat16)
    values = jnp.dot(e_hidden, expert_out, preferred_element_type=jnp.float32)
    e_dpre = (
        jnp.dot(grads, expert_out.T, preferred_element_type=jnp.float32) * gelu_slope(e_pre)
    ).astype(jnp.bfloat16)
    returns = jnp.dot(e_dpre, expert_in.T, preferred_element_type=jnp.float32)
    grad_in = jnp.dot(inputs.T, e_dpre, preferred_element_type=jnp.float32)
    grad_out = jnp.dot(e_hidden.T, grads, preferred_element_type=jnp.float32)
    values, returns, grad_in, grad_out = (values, returns, grad_in, grad_out)
    back_both = dense_exchange(
        jnp.concatenate(
            [
                values.reshape(col_count, slot_cap, model_width).astype(jnp.bfloat16),
                returns.reshape(col_count, slot_cap, model_width).astype(jnp.bfloat16),
            ],
            axis=1,
        ),
        "col",
    ).astype(jnp.float32)
    back_v, back_d = back_both[:, :slot_cap], back_both[:, slot_cap:]
    flat_v = (
        back_v.reshape(EXPERTS, group_len, slot_cap, model_width)
        .sum(axis=1)
        .reshape(EXPERTS * slot_cap, model_width)
    )
    flat_d = (
        back_d.reshape(EXPERTS, group_len, slot_cap, model_width)
        .sum(axis=1)
        .reshape(EXPERTS * slot_cap, model_width)
    )
    lookup = chosen * slot_cap + placed
    moe_sum = (
        (weights_flat[:, None] * jnp.take(flat_v, lookup, axis=0))
        .reshape(block_len, 2, model_width)
        .sum(axis=1)
    )
    grad_sum = jnp.take(flat_d, lookup, axis=0).reshape(block_len, 2, model_width).sum(axis=1)
    layer_rows = (own_rows.astype(jnp.float32) + moe_sum).astype(jnp.bfloat16)
    grad_rows = (own_grad.astype(jnp.float32) + grad_sum).astype(jnp.bfloat16)
    out_both = unswap_blocks(jnp.stack([layer_rows, grad_rows]), row_count)
    layer_out, mixed_grad = out_both[0], out_both[1]
    expert_in_grad = lax.psum_scatter(
        grad_in.astype(jnp.bfloat16).astype(jnp.float32), "row", scatter_dimension=0, tiled=True
    ).astype(jnp.bfloat16)
    expert_out_grad = lax.psum_scatter(
        grad_out.astype(jnp.bfloat16).astype(jnp.float32), "row", scatter_dimension=1, tiled=True
    ).astype(jnp.bfloat16)
    cot_panel = gather_rows(mixed_grad, "col")
    hgrad_terms = jnp.dot(cot_panel, w_down.T, preferred_element_type=jnp.float32)
    down_grad = jnp.dot(hidden_full.T, cot_panel, preferred_element_type=jnp.float32).astype(
        jnp.bfloat16
    )
    hidden_grad = scatter_sum(hgrad_terms, "row")
    dpre_full = gather_rows((hidden_grad * gelu_slope(preact)).astype(jnp.bfloat16), "row")
    up_grad = jnp.dot(tok_panel.T, dpre_full, preferred_element_type=jnp.float32).astype(
        jnp.bfloat16
    )
    rows_in = dpre_full
    input_term = scatter_sum(jnp.dot(rows_in, w_up.T, preferred_element_type=jnp.float32), "col")
    tokens_grad = (mixed_grad.astype(jnp.float32) + input_term).astype(jnp.bfloat16)
    return (layer_out, tokens_grad, up_grad, down_grad, expert_in_grad, expert_out_grad)


def solution(mesh):
    in_specs = (
        P("col", "row"),
        P("row", "col"),
        P("col", "row"),
        P(None, "col"),
        P("col", None),
        P("col", None),
        P("col", None),
        P("col", "row"),
    )
    out_specs = (
        P("col", "row"),
        P("col", "row"),
        P("row", "col"),
        P("col", "row"),
        P("row", "col"),
        P("col", "row"),
    )
    return jax.shard_map(
        on_device, mesh=mesh, in_specs=in_specs, out_specs=out_specs, check_vma=False
    )
```

```python
import jax
import jax.numpy as jnp
from jax import lax
from jax.sharding import PartitionSpec as P

EXPERTS = 4


gelu_scale = 0.7978845608028654
gelu_cubic = 0.044715


def gelu_tanh(value):
    return 0.5 * value * (1.0 + jnp.tanh(gelu_scale * (value + gelu_cubic * value * value * value)))


def gelu_slope(value):
    inner = jnp.tanh(gelu_scale * (value + gelu_cubic * value * value * value))
    return 0.5 * (1.0 + inner) + 0.5 * value * (1.0 - inner * inner) * gelu_scale * (
        1.0 + 3.0 * gelu_cubic * value * value
    )


def slot_ranks(pairs):
    count = pairs.shape[-1]
    positions = jnp.arange(count, dtype=jnp.int32)
    earlier = positions[:, None] > positions[None, :]
    matching = pairs[..., :, None] == pairs[..., None, :]
    return jnp.sum((matching & earlier).astype(jnp.int32), axis=-1)


def gather_rows(part, axis_name):
    count = lax.axis_size(axis_name)
    spread = jnp.broadcast_to(part[None], (count,) + part.shape)
    got = lax.all_to_all(spread, axis_name, 0, 0, tiled=True)
    return got.reshape((count * part.shape[0],) + part.shape[1:])


def scatter_sum(terms, axis_name):
    count = lax.axis_size(axis_name)
    blocks = terms.astype(jnp.bfloat16).reshape((count, terms.shape[0] // count) + terms.shape[1:])
    got = lax.all_to_all(blocks, axis_name, 0, 0, tiled=True)
    return got.astype(jnp.float32).sum(axis=0)


def scatter_sum_cols(terms, axis_name):
    count = lax.axis_size(axis_name)
    got = lax.all_to_all(terms.astype(jnp.bfloat16), axis_name, 1, 0, tiled=True)
    return got.reshape((count, terms.shape[0], terms.shape[1] // count)).astype(jnp.float32).sum(axis=0)


def dense_exchange(payload, axis_name):
    shape = payload.shape
    flat = payload.reshape(shape[0], -1, 128)
    got = lax.all_to_all(flat, axis_name, 0, 0, tiled=True)
    return got.reshape(shape)


def swap_blocks(pair, count):
    arrays, tok, width = pair.shape
    block = tok // count
    parts = pair.reshape(arrays, count, block, width).transpose(1, 0, 2, 3)
    got = lax.all_to_all(parts.reshape(count, arrays * block, width), "row", 0, 0, tiled=True)
    got = got.reshape(count, arrays, block, width).transpose(1, 2, 0, 3)
    return got.reshape(arrays, block, count * width)


def unswap_blocks(pair, count):
    arrays, block, full = pair.shape
    width = full // count
    parts = pair.reshape(arrays, block, count, width).transpose(2, 0, 1, 3)
    got = lax.all_to_all(parts.reshape(count, arrays * block, width), "row", 0, 0, tiled=True)
    got = got.reshape(count, arrays, block, width).transpose(1, 0, 2, 3)
    return got.reshape(arrays, count * block, width)


def on_device(tokens, w_up, w_down, expert_in, expert_out, expert_ids, route_weights, out_grad):
    row_count = lax.axis_size("row")
    col_count = lax.axis_size("col")
    tok_col = tokens.shape[0]
    block_len = tok_col // row_count
    group_len = col_count // EXPERTS
    slot_cap = max(2, 3 * block_len // 4)
    model_width = expert_out.shape[1]
    my_row = lax.axis_index("row")
    tok_panel = gather_rows(tokens, "col")
    up_terms = jnp.dot(tok_panel, w_up, preferred_element_type=jnp.float32)
    preact = scatter_sum(up_terms, "row")
    hidden_full = gather_rows(gelu_tanh(preact).astype(jnp.bfloat16), "row")
    rows_in = hidden_full
    dense_term = scatter_sum(jnp.dot(rows_in, w_down, preferred_element_type=jnp.float32), "col")
    mixed_act = (tokens.astype(jnp.float32) + dense_term).astype(jnp.bfloat16)
    own_both = swap_blocks(jnp.stack([mixed_act, out_grad]), row_count)
    own_rows, own_grad = own_both[0], own_both[1]
    ids_own = lax.dynamic_slice_in_dim(expert_ids, my_row * block_len, block_len, 0)
    weights_own = lax.dynamic_slice_in_dim(route_weights, my_row * block_len, block_len, 0)
    expert_range = jnp.arange(EXPERTS, dtype=jnp.int32)
    weight_table = jnp.sum(
        weights_own.astype(jnp.float32)[None, :, :]
        * (ids_own[None, :, :] == expert_range[:, None, None]).astype(jnp.float32),
        axis=2,
    )
    scaled = (weight_table[:, :, None] * own_grad.astype(jnp.float32)[None]).astype(jnp.bfloat16)
    per_expert = jnp.concatenate(
        [jnp.broadcast_to(own_rows[None], (EXPERTS,) + own_rows.shape), scaled], axis=1
    )
    payload = jnp.broadcast_to(
        per_expert[:, None], (EXPERTS, group_len) + per_expert.shape[1:]
    ).reshape(col_count, 2 * block_len, model_width)
    got = lax.all_to_all(payload, "col", 0, 0, tiled=True)
    got_flat = got.reshape(col_count * 2 * block_len, model_width)
    pre_full = jnp.dot(got_flat, expert_in, preferred_element_type=jnp.float32)
    gdot_full = jnp.dot(got_flat, expert_out.T, preferred_element_type=jnp.float32)
    hid_units = expert_in.shape[1]
    e_pre = pre_full.reshape(col_count, 2 * block_len, hid_units)[:, :block_len]
    g_dot = gdot_full.reshape(col_count, 2 * block_len, hid_units)[:, block_len:]
    e_hidden = gelu_tanh(e_pre).astype(jnp.bfloat16)
    e_dpre = (g_dot * gelu_slope(e_pre)).astype(jnp.bfloat16)
    blank = jnp.zeros_like(e_hidden)

    def at_rows(value, first):
        halves = [value, blank] if first else [blank, value]
        return jnp.concatenate(halves, axis=1).reshape(col_count * 2 * block_len, hid_units)

    back_flat = jnp.dot(
        at_rows(e_hidden, True), expert_out, preferred_element_type=jnp.float32
    ) + jnp.dot(at_rows(e_dpre, False), expert_in.T, preferred_element_type=jnp.float32)
    grad_in = jnp.dot(got_flat.T, at_rows(e_dpre, True), preferred_element_type=jnp.float32)
    grad_out = jnp.dot(at_rows(e_hidden, False).T, got_flat, preferred_element_type=jnp.float32)
    back = lax.all_to_all(
        back_flat.astype(jnp.bfloat16).reshape(col_count, 2 * block_len, model_width),
        "col",
        0,
        0,
        tiled=True,
    ).astype(jnp.float32)
    source_weights = jnp.repeat(weight_table, group_len, axis=0)
    moe_sum = jnp.sum(source_weights[:, :, None] * back[:, :block_len], axis=0)
    grad_sum = jnp.sum(back[:, block_len:], axis=0)
    layer_rows = (own_rows.astype(jnp.float32) + moe_sum).astype(jnp.bfloat16)
    grad_rows = (own_grad.astype(jnp.float32) + grad_sum).astype(jnp.bfloat16)
    out_both = unswap_blocks(jnp.stack([layer_rows, grad_rows]), row_count)
    layer_out, mixed_grad = out_both[0], out_both[1]
    expert_in_grad = lax.psum_scatter(
        grad_in.astype(jnp.bfloat16).astype(jnp.float32), "row", scatter_dimension=0, tiled=True
    ).astype(jnp.bfloat16)
    expert_out_grad = lax.psum_scatter(
        grad_out.astype(jnp.bfloat16).astype(jnp.float32), "row", scatter_dimension=1, tiled=True
    ).astype(jnp.bfloat16)
    cot_panel = gather_rows(mixed_grad, "col")
    hgrad_terms = jnp.dot(cot_panel, w_down.T, preferred_element_type=jnp.float32)
    down_grad = jnp.dot(hidden_full.T, cot_panel, preferred_element_type=jnp.float32).astype(
        jnp.bfloat16
    )
    hidden_grad = scatter_sum(hgrad_terms, "row")
    dpre_full = gather_rows((hidden_grad * gelu_slope(preact)).astype(jnp.bfloat16), "row")
    up_grad = jnp.dot(tok_panel.T, dpre_full, preferred_element_type=jnp.float32).astype(
        jnp.bfloat16
    )
    rows_in = dpre_full
    input_term = scatter_sum(jnp.dot(rows_in, w_up.T, preferred_element_type=jnp.float32), "col")
    tokens_grad = (mixed_grad.astype(jnp.float32) + input_term).astype(jnp.bfloat16)
    return (layer_out, tokens_grad, up_grad, down_grad, expert_in_grad, expert_out_grad)


def solution(mesh):
    in_specs = (
        P("col", "row"),
        P("row", "col"),
        P("col", "row"),
        P(None, "col"),
        P("col", None),
        P("col", None),
        P("col", None),
        P("col", "row"),
    )
    out_specs = (
        P("col", "row"),
        P("col", "row"),
        P("row", "col"),
        P("col", "row"),
        P("row", "col"),
        P("col", "row"),
    )
    return jax.shard_map(
        on_device, mesh=mesh, in_specs=in_specs, out_specs=out_specs, check_vma=False
    )
```

```python
import jax
import jax.numpy as jnp
from jax import lax
from jax.sharding import PartitionSpec as P

EXPERTS = 4


gelu_scale = 0.7978845608028654
gelu_cubic = 0.044715


def gelu_tanh(value):
    return 0.5 * value * (1.0 + jnp.tanh(gelu_scale * (value + gelu_cubic * value * value * value)))


def gelu_slope(value):
    inner = jnp.tanh(gelu_scale * (value + gelu_cubic * value * value * value))
    return 0.5 * (1.0 + inner) + 0.5 * value * (1.0 - inner * inner) * gelu_scale * (
        1.0 + 3.0 * gelu_cubic * value * value
    )


def slot_ranks(pairs):
    count = pairs.shape[-1]
    positions = jnp.arange(count, dtype=jnp.int32)
    earlier = positions[:, None] > positions[None, :]
    matching = pairs[..., :, None] == pairs[..., None, :]
    return jnp.sum((matching & earlier).astype(jnp.int32), axis=-1)


def gather_rows(part, axis_name):
    count = lax.axis_size(axis_name)
    spread = jnp.broadcast_to(part[None], (count,) + part.shape)
    got = lax.all_to_all(spread, axis_name, 0, 0, tiled=True)
    return got.reshape((count * part.shape[0],) + part.shape[1:])


def scatter_sum(terms, axis_name):
    count = lax.axis_size(axis_name)
    blocks = terms.astype(jnp.bfloat16).reshape((count, terms.shape[0] // count) + terms.shape[1:])
    got = lax.all_to_all(blocks, axis_name, 0, 0, tiled=True)
    return got.astype(jnp.float32).sum(axis=0)


def scatter_sum_cols(terms, axis_name):
    count = lax.axis_size(axis_name)
    got = lax.all_to_all(terms.astype(jnp.bfloat16), axis_name, 1, 0, tiled=True)
    return got.reshape((count, terms.shape[0], terms.shape[1] // count)).astype(jnp.float32).sum(axis=0)


def dense_exchange(payload, axis_name):
    shape = payload.shape
    flat = payload.reshape(shape[0], -1, 128)
    got = lax.all_to_all(flat, axis_name, 0, 0, tiled=True)
    return got.reshape(shape)


def swap_blocks(pair, count):
    arrays, tok, width = pair.shape
    block = tok // count
    parts = pair.reshape(arrays, count, block, width).transpose(1, 0, 2, 3)
    got = lax.all_to_all(parts.reshape(count, arrays * block, width), "row", 0, 0, tiled=True)
    got = got.reshape(count, arrays, block, width).transpose(1, 2, 0, 3)
    return got.reshape(arrays, block, count * width)


def unswap_blocks(pair, count):
    arrays, block, full = pair.shape
    width = full // count
    parts = pair.reshape(arrays, block, count, width).transpose(2, 0, 1, 3)
    got = lax.all_to_all(parts.reshape(count, arrays * block, width), "row", 0, 0, tiled=True)
    got = got.reshape(count, arrays, block, width).transpose(1, 0, 2, 3)
    return got.reshape(arrays, count * block, width)


def on_device(tokens, w_up, w_down, expert_in, expert_out, expert_ids, route_weights, out_grad):
    row_count = lax.axis_size("row")
    col_count = lax.axis_size("col")
    tok_col = tokens.shape[0]
    block_len = tok_col // row_count
    group_len = col_count // EXPERTS
    slot_cap = max(2, 3 * block_len // 4)
    model_width = expert_out.shape[1]
    my_row = lax.axis_index("row")
    tok_panel = gather_rows(tokens, "col")
    own_grad = swap_blocks(out_grad[None], row_count)[0]
    ids_own = lax.dynamic_slice_in_dim(expert_ids, my_row * block_len, block_len, 0)
    weights_own = lax.dynamic_slice_in_dim(route_weights, my_row * block_len, block_len, 0)
    expert_range = jnp.arange(EXPERTS, dtype=jnp.int32)
    weight_table = jnp.sum(
        weights_own.astype(jnp.float32)[None, :, :]
        * (ids_own[None, :, :] == expert_range[:, None, None]).astype(jnp.float32),
        axis=2,
    )
    table_row = jnp.pad(
        weight_table.reshape(1, EXPERTS * block_len).astype(jnp.bfloat16),
        ((0, 0), (0, model_width - EXPERTS * block_len)),
    )
    grad_pack = jnp.concatenate([own_grad, table_row], axis=0)
    tok_panel, grad_pack = lax.optimization_barrier((tok_panel, grad_pack))
    pack_all = lax.all_gather(grad_pack, "col", axis=0, tiled=False)
    my_expert = lax.axis_index("col") // group_len
    weights_recv = lax.dynamic_slice_in_dim(
        pack_all[:, block_len, : EXPERTS * block_len], my_expert * block_len, block_len, 1
    )
    grad_rows_in = (
        weights_recv.astype(jnp.float32)[:, :, None] * pack_all[:, :block_len].astype(jnp.float32)
    ).astype(jnp.bfloat16)
    up_terms = jnp.dot(tok_panel, w_up, preferred_element_type=jnp.float32)
    preact = scatter_sum(up_terms, "row")
    hidden_full = gather_rows(gelu_tanh(preact).astype(jnp.bfloat16), "row")
    rows_in = hidden_full
    dense_term = scatter_sum(jnp.dot(rows_in, w_down, preferred_element_type=jnp.float32), "col")
    mixed_act = (tokens.astype(jnp.float32) + dense_term).astype(jnp.bfloat16)
    own_rows = swap_blocks(mixed_act[None], row_count)[0]
    scaled_flat = grad_rows_in.reshape(col_count * block_len, model_width)
    payload = jnp.broadcast_to(own_rows[None], (col_count,) + own_rows.shape)
    got = lax.all_to_all(payload, "col", 0, 0, tiled=True)
    got_flat = got.reshape(col_count * block_len, model_width)
    hid_units = expert_in.shape[1]
    e_pre = jnp.dot(got_flat, expert_in, preferred_element_type=jnp.float32).reshape(
        col_count, block_len, hid_units
    )
    g_dot = jnp.dot(scaled_flat, expert_out.T, preferred_element_type=jnp.float32).reshape(
        col_count, block_len, hid_units
    )
    e_hidden = gelu_tanh(e_pre).astype(jnp.bfloat16)
    e_dpre = (g_dot * gelu_slope(e_pre)).astype(jnp.bfloat16)
    blank = jnp.zeros_like(e_hidden)

    def at_rows(value, first):
        halves = [value, blank] if first else [blank, value]
        return jnp.concatenate(halves, axis=1).reshape(col_count * 2 * block_len, hid_units)

    back_flat = jnp.dot(
        at_rows(e_hidden, True), expert_out, preferred_element_type=jnp.float32
    ) + jnp.dot(at_rows(e_dpre, False), expert_in.T, preferred_element_type=jnp.float32)
    grad_in = jnp.dot(
        got_flat.T, e_dpre.reshape(col_count * block_len, hid_units), preferred_element_type=jnp.float32
    )
    grad_out = jnp.dot(
        e_hidden.reshape(col_count * block_len, hid_units).T, scaled_flat, preferred_element_type=jnp.float32
    )
    back = lax.all_to_all(
        back_flat.astype(jnp.bfloat16).reshape(col_count, 2 * block_len, model_width),
        "col",
        0,
        0,
        tiled=True,
    ).astype(jnp.float32)
    source_weights = jnp.repeat(weight_table, group_len, axis=0)
    moe_sum = jnp.sum(source_weights[:, :, None] * back[:, :block_len], axis=0)
    grad_sum = jnp.sum(back[:, block_len:], axis=0)
    layer_rows = (own_rows.astype(jnp.float32) + moe_sum).astype(jnp.bfloat16)
    grad_rows = (own_grad.astype(jnp.float32) + grad_sum).astype(jnp.bfloat16)
    out_both = unswap_blocks(jnp.stack([layer_rows, grad_rows]), row_count)
    layer_out, mixed_grad = out_both[0], out_both[1]
    expert_in_grad = lax.psum_scatter(
        grad_in.astype(jnp.bfloat16).astype(jnp.float32), "row", scatter_dimension=0, tiled=True
    ).astype(jnp.bfloat16)
    expert_out_grad = lax.psum_scatter(
        grad_out.astype(jnp.bfloat16).astype(jnp.float32), "row", scatter_dimension=1, tiled=True
    ).astype(jnp.bfloat16)
    cot_panel = gather_rows(mixed_grad, "col")
    hgrad_terms = jnp.dot(cot_panel, w_down.T, preferred_element_type=jnp.float32)
    down_grad = jnp.dot(hidden_full.T, cot_panel, preferred_element_type=jnp.float32).astype(
        jnp.bfloat16
    )
    hidden_grad = scatter_sum(hgrad_terms, "row")
    dpre_full = gather_rows((hidden_grad * gelu_slope(preact)).astype(jnp.bfloat16), "row")
    up_grad = jnp.dot(tok_panel.T, dpre_full, preferred_element_type=jnp.float32).astype(
        jnp.bfloat16
    )
    rows_in = dpre_full
    input_term = scatter_sum(jnp.dot(rows_in, w_up.T, preferred_element_type=jnp.float32), "col")
    tokens_grad = (mixed_grad.astype(jnp.float32) + input_term).astype(jnp.bfloat16)
    return (layer_out, tokens_grad, up_grad, down_grad, expert_in_grad, expert_out_grad)


def solution(mesh):
    in_specs = (
        P("col", "row"),
        P("row", "col"),
        P("col", "row"),
        P(None, "col"),
        P("col", None),
        P("col", None),
        P("col", None),
        P("col", "row"),
    )
    out_specs = (
        P("col", "row"),
        P("col", "row"),
        P("row", "col"),
        P("col", "row"),
        P("row", "col"),
        P("col", "row"),
    )
    return jax.shard_map(
        on_device, mesh=mesh, in_specs=in_specs, out_specs=out_specs, check_vma=False
    )
```

```python
import jax
import jax.numpy as jnp
from jax import lax
from jax.sharding import PartitionSpec as P

EXPERTS = 4


gelu_scale = 0.7978845608028654
gelu_cubic = 0.044715


def gelu_tanh(value):
    return 0.5 * value * (1.0 + jnp.tanh(gelu_scale * (value + gelu_cubic * value * value * value)))


def gelu_slope(value):
    inner = jnp.tanh(gelu_scale * (value + gelu_cubic * value * value * value))
    return 0.5 * (1.0 + inner) + 0.5 * value * (1.0 - inner * inner) * gelu_scale * (
        1.0 + 3.0 * gelu_cubic * value * value
    )


def slot_ranks(pairs):
    count = pairs.shape[-1]
    positions = jnp.arange(count, dtype=jnp.int32)
    earlier = positions[:, None] > positions[None, :]
    matching = pairs[..., :, None] == pairs[..., None, :]
    return jnp.sum((matching & earlier).astype(jnp.int32), axis=-1)


def gather_rows(part, axis_name):
    count = lax.axis_size(axis_name)
    spread = jnp.broadcast_to(part[None], (count,) + part.shape)
    got = lax.all_to_all(spread, axis_name, 0, 0, tiled=True)
    return got.reshape((count * part.shape[0],) + part.shape[1:])


def scatter_sum(terms, axis_name):
    count = lax.axis_size(axis_name)
    blocks = terms.astype(jnp.bfloat16).reshape((count, terms.shape[0] // count) + terms.shape[1:])
    got = lax.all_to_all(blocks, axis_name, 0, 0, tiled=True)
    return got.astype(jnp.float32).sum(axis=0)


def scatter_sum_cols(terms, axis_name):
    count = lax.axis_size(axis_name)
    got = lax.all_to_all(terms.astype(jnp.bfloat16), axis_name, 1, 0, tiled=True)
    return got.reshape((count, terms.shape[0], terms.shape[1] // count)).astype(jnp.float32).sum(axis=0)


def dense_exchange(payload, axis_name):
    shape = payload.shape
    flat = payload.reshape(shape[0], -1, 128)
    got = lax.all_to_all(flat, axis_name, 0, 0, tiled=True)
    return got.reshape(shape)


def swap_blocks(pair, count):
    arrays, tok, width = pair.shape
    block = tok // count
    parts = pair.reshape(arrays, count, block, width).transpose(1, 0, 2, 3)
    got = lax.all_to_all(parts.reshape(count, arrays * block, width), "row", 0, 0, tiled=True)
    got = got.reshape(count, arrays, block, width).transpose(1, 2, 0, 3)
    return got.reshape(arrays, block, count * width)


def unswap_blocks(pair, count):
    arrays, block, full = pair.shape
    width = full // count
    parts = pair.reshape(arrays, block, count, width).transpose(2, 0, 1, 3)
    got = lax.all_to_all(parts.reshape(count, arrays * block, width), "row", 0, 0, tiled=True)
    got = got.reshape(count, arrays, block, width).transpose(1, 0, 2, 3)
    return got.reshape(arrays, count * block, width)


def on_device(tokens, w_up, w_down, expert_in, expert_out, expert_ids, route_weights, out_grad):
    row_count = lax.axis_size("row")
    col_count = lax.axis_size("col")
    tok_col = tokens.shape[0]
    block_len = tok_col // row_count
    group_len = col_count // EXPERTS
    slot_cap = max(2, 3 * block_len // 4)
    model_width = expert_out.shape[1]
    my_row = lax.axis_index("row")
    tok_panel = gather_rows(tokens, "col")
    own_grad = swap_blocks(out_grad[None], row_count)[0]
    ids_own = lax.dynamic_slice_in_dim(expert_ids, my_row * block_len, block_len, 0)
    weights_own = lax.dynamic_slice_in_dim(route_weights, my_row * block_len, block_len, 0)
    expert_range = jnp.arange(EXPERTS, dtype=jnp.int32)
    weight_table = jnp.sum(
        weights_own.astype(jnp.float32)[None, :, :]
        * (ids_own[None, :, :] == expert_range[:, None, None]).astype(jnp.float32),
        axis=2,
    )
    table_row = jnp.pad(
        weight_table.reshape(1, EXPERTS * block_len).astype(jnp.bfloat16),
        ((0, 0), (0, model_width - EXPERTS * block_len)),
    )
    grad_pack = jnp.concatenate([own_grad, table_row], axis=0)
    tok_panel, grad_pack = lax.optimization_barrier((tok_panel, grad_pack))
    pack_all = lax.all_gather(grad_pack, "col", axis=0, tiled=False)
    my_expert = lax.axis_index("col") // group_len
    weights_recv = lax.dynamic_slice_in_dim(
        pack_all[:, block_len, : EXPERTS * block_len], my_expert * block_len, block_len, 1
    )
    grad_rows_in = (
        weights_recv.astype(jnp.float32)[:, :, None] * pack_all[:, :block_len].astype(jnp.float32)
    ).astype(jnp.bfloat16)
    up_terms = jnp.dot(tok_panel, w_up, preferred_element_type=jnp.float32)
    preact = scatter_sum(up_terms, "row")
    hidden_full = gather_rows(gelu_tanh(preact).astype(jnp.bfloat16), "row")
    rows_in = hidden_full
    dense_term = scatter_sum(jnp.dot(rows_in, w_down, preferred_element_type=jnp.float32), "col")
    mixed_act = (tokens.astype(jnp.float32) + dense_term).astype(jnp.bfloat16)
    own_rows = swap_blocks(mixed_act[None], row_count)[0]
    scaled_flat = grad_rows_in.reshape(col_count * block_len, model_width)
    payload = jnp.broadcast_to(own_rows[None], (col_count,) + own_rows.shape)
    got = lax.all_to_all(payload, "col", 0, 0, tiled=True)
    got_flat = got.reshape(col_count * block_len, model_width)
    hid_units = expert_in.shape[1]
    e_pre = jnp.dot(got_flat, expert_in, preferred_element_type=jnp.float32).reshape(
        col_count, block_len, hid_units
    )
    g_dot = jnp.dot(scaled_flat, expert_out.T, preferred_element_type=jnp.float32).reshape(
        col_count, block_len, hid_units
    )
    e_hidden = gelu_tanh(e_pre).astype(jnp.bfloat16)
    e_dpre = (g_dot * gelu_slope(e_pre)).astype(jnp.bfloat16)
    blank = jnp.zeros_like(e_hidden)

    def at_rows(value, first):
        halves = [value, blank] if first else [blank, value]
        return jnp.concatenate(halves, axis=1).reshape(col_count * 2 * block_len, hid_units)

    back_flat = jnp.dot(
        at_rows(e_hidden, True), expert_out, preferred_element_type=jnp.float32
    ) + jnp.dot(at_rows(e_dpre, False), expert_in.T, preferred_element_type=jnp.float32)
    grad_in = jnp.dot(
        got_flat.T, e_dpre.reshape(col_count * block_len, hid_units), preferred_element_type=jnp.float32
    )
    grad_out = jnp.dot(
        e_hidden.reshape(col_count * block_len, hid_units).T, scaled_flat, preferred_element_type=jnp.float32
    )
    back = lax.all_to_all(
        back_flat.astype(jnp.bfloat16)
        .reshape(col_count, 2 * block_len, row_count, model_width // row_count)
        .transpose(2, 0, 1, 3)
        .reshape(row_count * col_count, 2 * block_len, model_width // row_count),
        ("row", "col"),
        0,
        0,
        tiled=True,
    ).astype(jnp.float32).reshape(row_count, col_count, 2 * block_len, model_width // row_count)
    local_table = jnp.sum(
        route_weights.astype(jnp.float32)[:, None, :]
        * (expert_ids[:, None, :] == expert_range[None, :, None]).astype(jnp.float32),
        axis=2,
    )
    source_weights = jnp.repeat(
        local_table.reshape(row_count, block_len, EXPERTS).transpose(0, 2, 1), group_len, axis=1
    )
    moe_sum = jnp.sum(source_weights[:, :, :, None] * back[:, :, :block_len], axis=1)
    grad_sum = jnp.sum(back[:, :, block_len:], axis=1)
    layer_out = (mixed_act.astype(jnp.float32) + moe_sum.reshape(tok_col, -1)).astype(jnp.bfloat16)
    mixed_grad = (out_grad.astype(jnp.float32) + grad_sum.reshape(tok_col, -1)).astype(jnp.bfloat16)
    expert_in_grad = lax.psum_scatter(
        grad_in.astype(jnp.bfloat16).astype(jnp.float32), "row", scatter_dimension=0, tiled=True
    ).astype(jnp.bfloat16)
    expert_out_grad = lax.psum_scatter(
        grad_out.astype(jnp.bfloat16).astype(jnp.float32), "row", scatter_dimension=1, tiled=True
    ).astype(jnp.bfloat16)
    cot_panel = gather_rows(mixed_grad, "col")
    hgrad_terms = jnp.dot(cot_panel, w_down.T, preferred_element_type=jnp.float32)
    down_grad = jnp.dot(hidden_full.T, cot_panel, preferred_element_type=jnp.float32).astype(
        jnp.bfloat16
    )
    hidden_grad = scatter_sum(hgrad_terms, "row")
    dpre_full = gather_rows((hidden_grad * gelu_slope(preact)).astype(jnp.bfloat16), "row")
    up_grad = jnp.dot(tok_panel.T, dpre_full, preferred_element_type=jnp.float32).astype(
        jnp.bfloat16
    )
    rows_in = dpre_full
    input_term = scatter_sum(jnp.dot(rows_in, w_up.T, preferred_element_type=jnp.float32), "col")
    tokens_grad = (mixed_grad.astype(jnp.float32) + input_term).astype(jnp.bfloat16)
    return (layer_out, tokens_grad, up_grad, down_grad, expert_in_grad, expert_out_grad)


def solution(mesh):
    in_specs = (
        P("col", "row"),
        P("row", "col"),
        P("col", "row"),
        P(None, "col"),
        P("col", None),
        P("col", None),
        P("col", None),
        P("col", "row"),
    )
    out_specs = (
        P("col", "row"),
        P("col", "row"),
        P("row", "col"),
        P("col", "row"),
        P("row", "col"),
        P("col", "row"),
    )
    return jax.shard_map(
        on_device, mesh=mesh, in_specs=in_specs, out_specs=out_specs, check_vma=False
    )
```

```python
import jax
import jax.numpy as jnp
from jax import lax
from jax.sharding import Mesh, PartitionSpec as P

EXPERTS = 4
COL = ("cy", "cz")


gelu_scale = 0.7978845608028654
gelu_cubic = 0.044715


def gelu_tanh(value):
    return 0.5 * value * (1.0 + jnp.tanh(gelu_scale * (value + gelu_cubic * value * value * value)))


def gelu_slope(value):
    inner = jnp.tanh(gelu_scale * (value + gelu_cubic * value * value * value))
    return 0.5 * (1.0 + inner) + 0.5 * value * (1.0 - inner * inner) * gelu_scale * (
        1.0 + 3.0 * gelu_cubic * value * value
    )


def slot_ranks(pairs):
    count = pairs.shape[-1]
    positions = jnp.arange(count, dtype=jnp.int32)
    earlier = positions[:, None] > positions[None, :]
    matching = pairs[..., :, None] == pairs[..., None, :]
    return jnp.sum((matching & earlier).astype(jnp.int32), axis=-1)


def gather_rows(part, axis_name):
    count = lax.axis_size(axis_name)
    spread = jnp.broadcast_to(part[None], (count,) + part.shape)
    got = lax.all_to_all(spread, axis_name, 0, 0, tiled=True)
    return got.reshape((count * part.shape[0],) + part.shape[1:])


def scatter_sum(terms, axis_name):
    count = lax.axis_size(axis_name)
    blocks = terms.astype(jnp.bfloat16).reshape((count, terms.shape[0] // count) + terms.shape[1:])
    got = lax.all_to_all(blocks, axis_name, 0, 0, tiled=True)
    return got.astype(jnp.float32).sum(axis=0)


def scatter_sum_cols(terms, axis_name):
    count = lax.axis_size(axis_name)
    got = lax.all_to_all(terms.astype(jnp.bfloat16), axis_name, 1, 0, tiled=True)
    return got.reshape((count, terms.shape[0], terms.shape[1] // count)).astype(jnp.float32).sum(axis=0)


def dense_exchange(payload, axis_name):
    shape = payload.shape
    flat = payload.reshape(shape[0], -1, 128)
    got = lax.all_to_all(flat, axis_name, 0, 0, tiled=True)
    return got.reshape(shape)


def swap_blocks(pair, count):
    arrays, tok, width = pair.shape
    block = tok // count
    parts = pair.reshape(arrays, count, block, width).transpose(1, 0, 2, 3)
    got = lax.all_to_all(parts.reshape(count, arrays * block, width), "row", 0, 0, tiled=True)
    got = got.reshape(count, arrays, block, width).transpose(1, 2, 0, 3)
    return got.reshape(arrays, block, count * width)


def unswap_blocks(pair, count):
    arrays, block, full = pair.shape
    width = full // count
    parts = pair.reshape(arrays, block, count, width).transpose(2, 0, 1, 3)
    got = lax.all_to_all(parts.reshape(count, arrays * block, width), "row", 0, 0, tiled=True)
    got = got.reshape(count, arrays, block, width).transpose(1, 0, 2, 3)
    return got.reshape(arrays, count * block, width)


def on_device(tokens, w_up, w_down, expert_in, expert_out, expert_ids, route_weights, out_grad):
    row_count = lax.axis_size("row")
    col_count = lax.axis_size("cy") * lax.axis_size("cz")
    tok_col = tokens.shape[0]
    block_len = tok_col // row_count
    group_len = col_count // EXPERTS
    slot_cap = max(2, 3 * block_len // 4)
    model_width = expert_out.shape[1]
    my_row = lax.axis_index("row")
    tok_panel = gather_rows(tokens, COL)
    own_grad = swap_blocks(out_grad[None], row_count)[0]
    ids_own = lax.dynamic_slice_in_dim(expert_ids, my_row * block_len, block_len, 0)
    weights_own = lax.dynamic_slice_in_dim(route_weights, my_row * block_len, block_len, 0)
    expert_range = jnp.arange(EXPERTS, dtype=jnp.int32)
    weight_table = jnp.sum(
        weights_own.astype(jnp.float32)[None, :, :]
        * (ids_own[None, :, :] == expert_range[:, None, None]).astype(jnp.float32),
        axis=2,
    )
    table_row = jnp.pad(
        weight_table.reshape(1, EXPERTS * block_len).astype(jnp.bfloat16),
        ((0, 0), (0, model_width - EXPERTS * block_len)),
    )
    grad_pack = jnp.concatenate([own_grad, table_row], axis=0)
    tok_panel, grad_pack = lax.optimization_barrier((tok_panel, grad_pack))
    pack_all = lax.all_gather(grad_pack, COL, axis=0, tiled=False)
    my_expert = lax.axis_index(COL) // group_len
    weights_recv = lax.dynamic_slice_in_dim(
        pack_all[:, block_len, : EXPERTS * block_len], my_expert * block_len, block_len, 1
    )
    grad_rows_in = (
        weights_recv.astype(jnp.float32)[:, :, None] * pack_all[:, :block_len].astype(jnp.float32)
    ).astype(jnp.bfloat16)
    up_terms = jnp.dot(tok_panel, w_up, preferred_element_type=jnp.float32)
    preact = scatter_sum(up_terms, "row")
    hidden_full = gather_rows(gelu_tanh(preact).astype(jnp.bfloat16), "row")
    rows_in = hidden_full
    dense_term = scatter_sum(jnp.dot(rows_in, w_down, preferred_element_type=jnp.float32), COL)
    mixed_act = (tokens.astype(jnp.float32) + dense_term).astype(jnp.bfloat16)
    own_rows = swap_blocks(mixed_act[None], row_count)[0]
    scaled_flat = grad_rows_in.reshape(col_count * block_len, model_width)
    payload = jnp.broadcast_to(own_rows[None], (col_count,) + own_rows.shape)
    got = lax.all_to_all(payload, COL, 0, 0, tiled=True)
    got_flat = got.reshape(col_count * block_len, model_width)
    hid_units = expert_in.shape[1]
    e_pre = jnp.dot(got_flat, expert_in, preferred_element_type=jnp.float32).reshape(
        col_count, block_len, hid_units
    )
    g_dot = jnp.dot(scaled_flat, expert_out.T, preferred_element_type=jnp.float32).reshape(
        col_count, block_len, hid_units
    )
    e_hidden = gelu_tanh(e_pre).astype(jnp.bfloat16)
    e_dpre = (g_dot * gelu_slope(e_pre)).astype(jnp.bfloat16)
    blank = jnp.zeros_like(e_hidden)

    def at_rows(value, first):
        halves = [value, blank] if first else [blank, value]
        return jnp.concatenate(halves, axis=1).reshape(col_count * 2 * block_len, hid_units)

    value_terms = weights_recv.astype(jnp.float32).reshape(col_count * block_len, 1) * jnp.dot(
        e_hidden.reshape(col_count * block_len, hid_units), expert_out, preferred_element_type=jnp.float32
    )
    returns = jnp.dot(
        e_dpre.reshape(col_count * block_len, hid_units), expert_in.T, preferred_element_type=jnp.float32
    )
    grad_in = jnp.dot(
        got_flat.T, e_dpre.reshape(col_count * block_len, hid_units), preferred_element_type=jnp.float32
    )
    grad_out = jnp.dot(
        e_hidden.reshape(col_count * block_len, hid_units).T, scaled_flat, preferred_element_type=jnp.float32
    )
    y_count = lax.axis_size("cy")
    z_count = lax.axis_size("cz")
    by_z = value_terms.reshape(y_count, z_count, block_len, model_width).transpose(1, 0, 2, 3)
    value_part = lax.psum_scatter(by_z, "cz", scatter_dimension=0, tiled=True)
    back = lax.all_to_all(
        returns.astype(jnp.bfloat16).reshape(col_count, block_len, model_width), COL, 0, 0, tiled=True
    ).astype(jnp.float32)
    grad_sum = jnp.sum(back, axis=0)
    grad_rows = (own_grad.astype(jnp.float32) + grad_sum).astype(jnp.bfloat16)
    mixed_grad = unswap_blocks(grad_rows[None], row_count)[0]
    expert_in_grad = lax.psum_scatter(
        grad_in.astype(jnp.bfloat16).astype(jnp.float32), "row", scatter_dimension=0, tiled=True
    ).astype(jnp.bfloat16)
    expert_out_grad = lax.psum_scatter(
        grad_out.astype(jnp.bfloat16).astype(jnp.float32), "row", scatter_dimension=1, tiled=True
    ).astype(jnp.bfloat16)
    cot_panel = gather_rows(mixed_grad, COL)
    value_part, cot_panel = lax.optimization_barrier((value_part, cot_panel))
    hgrad_terms = jnp.dot(cot_panel, w_down.T, preferred_element_type=jnp.float32)
    down_grad = jnp.dot(hidden_full.T, cot_panel, preferred_element_type=jnp.float32).astype(
        jnp.bfloat16
    )
    hidden_grad = scatter_sum(hgrad_terms, "row")
    value_all = lax.all_gather(value_part[0], "cy", axis=0, tiled=False)
    moe_sum = jnp.sum(
        lax.dynamic_index_in_dim(value_all, lax.axis_index("cy"), 1, keepdims=False), axis=0
    )
    layer_rows = (own_rows.astype(jnp.float32) + moe_sum).astype(jnp.bfloat16)
    layer_out = unswap_blocks(layer_rows[None], row_count)[0]
    dpre_full = gather_rows((hidden_grad * gelu_slope(preact)).astype(jnp.bfloat16), "row")
    up_grad = jnp.dot(tok_panel.T, dpre_full, preferred_element_type=jnp.float32).astype(
        jnp.bfloat16
    )
    rows_in = dpre_full
    input_term = scatter_sum(jnp.dot(rows_in, w_up.T, preferred_element_type=jnp.float32), COL)
    tokens_grad = (mixed_grad.astype(jnp.float32) + input_term).astype(jnp.bfloat16)
    return (layer_out, tokens_grad, up_grad, down_grad, expert_in_grad, expert_out_grad)


def solution(mesh):
    in_specs = (
        P(COL, "row"),
        P("row", COL),
        P(COL, "row"),
        P(None, COL),
        P(COL, None),
        P(COL, None),
        P(COL, None),
        P(COL, "row"),
    )
    out_specs = (
        P(COL, "row"),
        P(COL, "row"),
        P("row", COL),
        P(COL, "row"),
        P("row", COL),
        P(COL, "row"),
    )
    rows, cols = mesh.devices.shape
    split_mesh = Mesh(mesh.devices.reshape(rows, EXPERTS, cols // EXPERTS), ("row", "cy", "cz"))
    return jax.shard_map(
        on_device, mesh=split_mesh, in_specs=in_specs, out_specs=out_specs, check_vma=False
    )
```

```python
import jax
import jax.numpy as jnp
from jax import lax
from jax.sharding import Mesh, PartitionSpec as P

EXPERTS = 4
COL = ("cy", "cz")


gelu_scale = 0.7978845608028654
gelu_cubic = 0.044715


def gelu_tanh(value):
    return 0.5 * value * (1.0 + jnp.tanh(gelu_scale * (value + gelu_cubic * value * value * value)))


def gelu_slope(value):
    inner = jnp.tanh(gelu_scale * (value + gelu_cubic * value * value * value))
    return 0.5 * (1.0 + inner) + 0.5 * value * (1.0 - inner * inner) * gelu_scale * (
        1.0 + 3.0 * gelu_cubic * value * value
    )


def slot_ranks(pairs):
    count = pairs.shape[-1]
    positions = jnp.arange(count, dtype=jnp.int32)
    earlier = positions[:, None] > positions[None, :]
    matching = pairs[..., :, None] == pairs[..., None, :]
    return jnp.sum((matching & earlier).astype(jnp.int32), axis=-1)


def gather_rows(part, axis_name):
    count = lax.axis_size(axis_name)
    spread = jnp.broadcast_to(part[None], (count,) + part.shape)
    got = lax.all_to_all(spread, axis_name, 0, 0, tiled=True)
    return got.reshape((count * part.shape[0],) + part.shape[1:])


def scatter_sum(terms, axis_name):
    count = lax.axis_size(axis_name)
    blocks = terms.astype(jnp.bfloat16).reshape((count, terms.shape[0] // count) + terms.shape[1:])
    got = lax.all_to_all(blocks, axis_name, 0, 0, tiled=True)
    return got.astype(jnp.float32).sum(axis=0)


def scatter_sum_cols(terms, axis_name):
    count = lax.axis_size(axis_name)
    got = lax.all_to_all(terms.astype(jnp.bfloat16), axis_name, 1, 0, tiled=True)
    return got.reshape((count, terms.shape[0], terms.shape[1] // count)).astype(jnp.float32).sum(axis=0)


def dense_exchange(payload, axis_name):
    shape = payload.shape
    flat = payload.reshape(shape[0], -1, 128)
    got = lax.all_to_all(flat, axis_name, 0, 0, tiled=True)
    return got.reshape(shape)


def swap_blocks(pair, count):
    arrays, tok, width = pair.shape
    block = tok // count
    parts = pair.reshape(arrays, count, block, width).transpose(1, 0, 2, 3)
    got = lax.all_to_all(parts.reshape(count, arrays * block, width), "row", 0, 0, tiled=True)
    got = got.reshape(count, arrays, block, width).transpose(1, 2, 0, 3)
    return got.reshape(arrays, block, count * width)


def unswap_blocks(pair, count):
    arrays, block, full = pair.shape
    width = full // count
    parts = pair.reshape(arrays, block, count, width).transpose(2, 0, 1, 3)
    got = lax.all_to_all(parts.reshape(count, arrays * block, width), "row", 0, 0, tiled=True)
    got = got.reshape(count, arrays, block, width).transpose(1, 0, 2, 3)
    return got.reshape(arrays, count * block, width)


def on_device(tokens, w_up, w_down, expert_in, expert_out, expert_ids, route_weights, out_grad):
    row_count = lax.axis_size("row")
    col_count = lax.axis_size("cy") * lax.axis_size("cz")
    tok_col = tokens.shape[0]
    block_len = tok_col // row_count
    group_len = col_count // EXPERTS
    slot_cap = max(2, 3 * block_len // 4)
    model_width = expert_out.shape[1]
    my_row = lax.axis_index("row")
    tok_panel = gather_rows(tokens, COL)
    own_grad = swap_blocks(out_grad[None], row_count)[0]
    ids_own = lax.dynamic_slice_in_dim(expert_ids, my_row * block_len, block_len, 0)
    weights_own = lax.dynamic_slice_in_dim(route_weights, my_row * block_len, block_len, 0)
    expert_range = jnp.arange(EXPERTS, dtype=jnp.int32)
    weight_table = jnp.sum(
        weights_own.astype(jnp.float32)[None, :, :]
        * (ids_own[None, :, :] == expert_range[:, None, None]).astype(jnp.float32),
        axis=2,
    )
    table_row = jnp.pad(
        weight_table.reshape(1, EXPERTS * block_len).astype(jnp.bfloat16),
        ((0, 0), (0, model_width - EXPERTS * block_len)),
    )
    grad_pack = jnp.concatenate([own_grad, table_row], axis=0)
    tok_panel, grad_pack = lax.optimization_barrier((tok_panel, grad_pack))
    pack_all = lax.all_gather(grad_pack, COL, axis=0, tiled=False)
    my_expert = lax.axis_index(COL) // group_len
    weights_recv = lax.dynamic_slice_in_dim(
        pack_all[:, block_len, : EXPERTS * block_len], my_expert * block_len, block_len, 1
    )
    grad_rows_in = (
        weights_recv.astype(jnp.float32)[:, :, None] * pack_all[:, :block_len].astype(jnp.float32)
    ).astype(jnp.bfloat16)
    up_terms = jnp.dot(tok_panel, w_up, preferred_element_type=jnp.float32)
    preact = scatter_sum(up_terms, "row")
    hidden_full = gather_rows(gelu_tanh(preact).astype(jnp.bfloat16), "row")
    rows_in = hidden_full
    dense_term = scatter_sum(jnp.dot(rows_in, w_down, preferred_element_type=jnp.float32), COL)
    mixed_act = (tokens.astype(jnp.float32) + dense_term).astype(jnp.bfloat16)
    own_rows = swap_blocks(mixed_act[None], row_count)[0]
    scaled_flat = grad_rows_in.reshape(col_count * block_len, model_width)
    payload = jnp.broadcast_to(own_rows[None], (col_count,) + own_rows.shape)
    got = lax.all_to_all(payload, COL, 0, 0, tiled=True)
    got_flat = got.reshape(col_count * block_len, model_width)
    hid_units = expert_in.shape[1]
    e_pre = jnp.dot(got_flat, expert_in, preferred_element_type=jnp.float32).reshape(
        col_count, block_len, hid_units
    )
    g_dot = jnp.dot(scaled_flat, expert_out.T, preferred_element_type=jnp.float32).reshape(
        col_count, block_len, hid_units
    )
    e_hidden = gelu_tanh(e_pre).astype(jnp.bfloat16)
    e_dpre = (g_dot * gelu_slope(e_pre)).astype(jnp.bfloat16)
    blank = jnp.zeros_like(e_hidden)

    def at_rows(value, first):
        halves = [value, blank] if first else [blank, value]
        return jnp.concatenate(halves, axis=1).reshape(col_count * 2 * block_len, hid_units)

    value_terms = weights_recv.astype(jnp.float32).reshape(col_count * block_len, 1) * jnp.dot(
        e_hidden.reshape(col_count * block_len, hid_units), expert_out, preferred_element_type=jnp.float32
    )
    returns = jnp.dot(
        e_dpre.reshape(col_count * block_len, hid_units), expert_in.T, preferred_element_type=jnp.float32
    )
    grad_in = jnp.dot(
        got_flat.T, e_dpre.reshape(col_count * block_len, hid_units), preferred_element_type=jnp.float32
    )
    grad_out = jnp.dot(
        e_hidden.reshape(col_count * block_len, hid_units).T, scaled_flat, preferred_element_type=jnp.float32
    )
    y_count = lax.axis_size("cy")
    z_count = lax.axis_size("cz")
    by_z = (
        value_terms.astype(jnp.bfloat16)
        .reshape(y_count, z_count, block_len, model_width)
        .transpose(1, 0, 2, 3)
    )
    value_part = lax.psum_scatter(by_z, "cz", scatter_dimension=0, tiled=True)
    back = lax.all_to_all(
        returns.astype(jnp.bfloat16).reshape(col_count, block_len, model_width), COL, 0, 0, tiled=True
    ).astype(jnp.float32)
    grad_sum = jnp.sum(back, axis=0)
    grad_rows = (own_grad.astype(jnp.float32) + grad_sum).astype(jnp.bfloat16)
    mixed_grad = unswap_blocks(grad_rows[None], row_count)[0]
    expert_in_grad = lax.psum_scatter(
        grad_in.astype(jnp.bfloat16).astype(jnp.float32), "row", scatter_dimension=0, tiled=True
    ).astype(jnp.bfloat16)
    expert_out_grad = lax.psum_scatter(
        grad_out.astype(jnp.bfloat16).astype(jnp.float32), "row", scatter_dimension=1, tiled=True
    ).astype(jnp.bfloat16)
    cot_panel = gather_rows(mixed_grad, COL)
    value_part, cot_panel = lax.optimization_barrier((value_part, cot_panel))
    hgrad_terms = jnp.dot(cot_panel, w_down.T, preferred_element_type=jnp.float32)
    down_grad = jnp.dot(hidden_full.T, cot_panel, preferred_element_type=jnp.float32).astype(
        jnp.bfloat16
    )
    hidden_grad = scatter_sum(hgrad_terms, "row")
    value_all = lax.all_gather(value_part[0], "cy", axis=0, tiled=False)
    moe_sum = jnp.sum(
        lax.dynamic_index_in_dim(value_all, lax.axis_index("cy"), 1, keepdims=False).astype(
            jnp.float32
        ),
        axis=0,
    )
    layer_rows = (own_rows.astype(jnp.float32) + moe_sum).astype(jnp.bfloat16)
    layer_out = unswap_blocks(layer_rows[None], row_count)[0]
    dpre_full = gather_rows((hidden_grad * gelu_slope(preact)).astype(jnp.bfloat16), "row")
    up_grad = jnp.dot(tok_panel.T, dpre_full, preferred_element_type=jnp.float32).astype(
        jnp.bfloat16
    )
    rows_in = dpre_full
    input_term = scatter_sum(jnp.dot(rows_in, w_up.T, preferred_element_type=jnp.float32), COL)
    tokens_grad = (mixed_grad.astype(jnp.float32) + input_term).astype(jnp.bfloat16)
    return (layer_out, tokens_grad, up_grad, down_grad, expert_in_grad, expert_out_grad)


def solution(mesh):
    in_specs = (
        P(COL, "row"),
        P("row", COL),
        P(COL, "row"),
        P(None, COL),
        P(COL, None),
        P(COL, None),
        P(COL, None),
        P(COL, "row"),
    )
    out_specs = (
        P(COL, "row"),
        P(COL, "row"),
        P("row", COL),
        P(COL, "row"),
        P("row", COL),
        P(COL, "row"),
    )
    rows, cols = mesh.devices.shape
    split_mesh = Mesh(mesh.devices.reshape(rows, EXPERTS, cols // EXPERTS), ("row", "cy", "cz"))
    return jax.shard_map(
        on_device, mesh=split_mesh, in_specs=in_specs, out_specs=out_specs, check_vma=False
    )
```

```python
import jax
import jax.numpy as jnp
from jax import lax
from jax.sharding import PartitionSpec as P

EXPERTS = 4


gelu_scale = 0.7978845608028654
gelu_cubic = 0.044715


def gelu_tanh(value):
    return 0.5 * value * (1.0 + jnp.tanh(gelu_scale * (value + gelu_cubic * value * value * value)))


def gelu_slope(value):
    inner = jnp.tanh(gelu_scale * (value + gelu_cubic * value * value * value))
    return 0.5 * (1.0 + inner) + 0.5 * value * (1.0 - inner * inner) * gelu_scale * (
        1.0 + 3.0 * gelu_cubic * value * value
    )


def slot_ranks(pairs):
    count = pairs.shape[-1]
    positions = jnp.arange(count, dtype=jnp.int32)
    earlier = positions[:, None] > positions[None, :]
    matching = pairs[..., :, None] == pairs[..., None, :]
    return jnp.sum((matching & earlier).astype(jnp.int32), axis=-1)


def gather_rows(part, axis_name):
    count = lax.axis_size(axis_name)
    spread = jnp.broadcast_to(part[None], (count,) + part.shape)
    got = lax.all_to_all(spread, axis_name, 0, 0, tiled=True)
    return got.reshape((count * part.shape[0],) + part.shape[1:])


def scatter_sum(terms, axis_name):
    count = lax.axis_size(axis_name)
    blocks = terms.astype(jnp.bfloat16).reshape((count, terms.shape[0] // count) + terms.shape[1:])
    got = lax.all_to_all(blocks, axis_name, 0, 0, tiled=True)
    return got.astype(jnp.float32).sum(axis=0)


def scatter_sum_cols(terms, axis_name):
    count = lax.axis_size(axis_name)
    got = lax.all_to_all(terms.astype(jnp.bfloat16), axis_name, 1, 0, tiled=True)
    return got.reshape((count, terms.shape[0], terms.shape[1] // count)).astype(jnp.float32).sum(axis=0)


def dense_exchange(payload, axis_name):
    shape = payload.shape
    flat = payload.reshape(shape[0], -1, 128)
    got = lax.all_to_all(flat, axis_name, 0, 0, tiled=True)
    return got.reshape(shape)


def swap_blocks(pair, count):
    arrays, tok, width = pair.shape
    block = tok // count
    parts = pair.reshape(arrays, count, block, width).transpose(1, 0, 2, 3)
    got = lax.all_to_all(parts.reshape(count, arrays * block, width), "row", 0, 0, tiled=True)
    got = got.reshape(count, arrays, block, width).transpose(1, 2, 0, 3)
    return got.reshape(arrays, block, count * width)


def unswap_blocks(pair, count):
    arrays, block, full = pair.shape
    width = full // count
    parts = pair.reshape(arrays, block, count, width).transpose(2, 0, 1, 3)
    got = lax.all_to_all(parts.reshape(count, arrays * block, width), "row", 0, 0, tiled=True)
    got = got.reshape(count, arrays, block, width).transpose(1, 0, 2, 3)
    return got.reshape(arrays, count * block, width)


def on_device(tokens, w_up, w_down, expert_in, expert_out, expert_ids, route_weights, out_grad):
    row_count = lax.axis_size("row")
    col_count = lax.axis_size("col")
    tok_col = tokens.shape[0]
    block_len = tok_col // row_count
    group_len = col_count // EXPERTS
    slot_cap = max(2, 3 * block_len // 4)
    model_width = expert_out.shape[1]
    my_row = lax.axis_index("row")
    own_grad = swap_blocks(out_grad[None], row_count)[0]
    ids_own = lax.dynamic_slice_in_dim(expert_ids, my_row * block_len, block_len, 0)
    weights_own = lax.dynamic_slice_in_dim(route_weights, my_row * block_len, block_len, 0)
    expert_range = jnp.arange(EXPERTS, dtype=jnp.int32)
    weight_table = jnp.sum(
        weights_own.astype(jnp.float32)[None, :, :]
        * (ids_own[None, :, :] == expert_range[:, None, None]).astype(jnp.float32),
        axis=2,
    )
    table_row = jnp.pad(
        weight_table.reshape(1, EXPERTS * block_len).astype(jnp.bfloat16),
        ((0, 0), (0, model_width - EXPERTS * block_len)),
    )
    grad_pack = jnp.concatenate([own_grad, table_row], axis=0)
    tokens_ready, grad_pack = lax.optimization_barrier((tokens, grad_pack))
    tok_panel = gather_rows(tokens_ready, "col")
    pack_all = lax.all_gather(grad_pack, "col", axis=0, tiled=False)
    my_expert = lax.axis_index("col") // group_len
    weights_recv = lax.dynamic_slice_in_dim(
        pack_all[:, block_len, : EXPERTS * block_len], my_expert * block_len, block_len, 1
    )
    grad_rows_in = (
        weights_recv.astype(jnp.float32)[:, :, None] * pack_all[:, :block_len].astype(jnp.float32)
    ).astype(jnp.bfloat16)
    up_terms = jnp.dot(tok_panel, w_up, preferred_element_type=jnp.float32)
    preact = scatter_sum(up_terms, "row")
    hidden_full = gather_rows(gelu_tanh(preact).astype(jnp.bfloat16), "row")
    hidden_full, pack_all = lax.optimization_barrier((hidden_full, pack_all))
    rows_in = hidden_full
    dense_term = scatter_sum(jnp.dot(rows_in, w_down, preferred_element_type=jnp.float32), "col")
    mixed_act = (tokens.astype(jnp.float32) + dense_term).astype(jnp.bfloat16)
    own_rows = swap_blocks(mixed_act[None], row_count)[0]
    scaled_flat = grad_rows_in.reshape(col_count * block_len, model_width)
    payload = jnp.broadcast_to(own_rows[None], (col_count,) + own_rows.shape)
    got = lax.all_to_all(payload, "col", 0, 0, tiled=True)
    got_flat = got.reshape(col_count * block_len, model_width)
    hid_units = expert_in.shape[1]
    e_pre = jnp.dot(got_flat, expert_in, preferred_element_type=jnp.float32).reshape(
        col_count, block_len, hid_units
    )
    g_dot = jnp.dot(scaled_flat, expert_out.T, preferred_element_type=jnp.float32).reshape(
        col_count, block_len, hid_units
    )
    e_hidden = gelu_tanh(e_pre).astype(jnp.bfloat16)
    e_dpre = (g_dot * gelu_slope(e_pre)).astype(jnp.bfloat16)
    blank = jnp.zeros_like(e_hidden)

    def at_rows(value, first):
        halves = [value, blank] if first else [blank, value]
        return jnp.concatenate(halves, axis=1).reshape(col_count * 2 * block_len, hid_units)

    back_flat = jnp.dot(
        at_rows(e_hidden, True), expert_out, preferred_element_type=jnp.float32
    ) + jnp.dot(at_rows(e_dpre, False), expert_in.T, preferred_element_type=jnp.float32)
    grad_in = jnp.dot(
        got_flat.T, e_dpre.reshape(col_count * block_len, hid_units), preferred_element_type=jnp.float32
    )
    grad_out = jnp.dot(
        e_hidden.reshape(col_count * block_len, hid_units).T, scaled_flat, preferred_element_type=jnp.float32
    )
    back = lax.all_to_all(
        back_flat.astype(jnp.bfloat16)
        .reshape(col_count, 2 * block_len, row_count, model_width // row_count)
        .transpose(2, 0, 1, 3)
        .reshape(row_count * col_count, 2 * block_len, model_width // row_count),
        ("row", "col"),
        0,
        0,
        tiled=True,
    ).astype(jnp.float32).reshape(row_count, col_count, 2 * block_len, model_width // row_count)
    local_table = jnp.sum(
        route_weights.astype(jnp.float32)[:, None, :]
        * (expert_ids[:, None, :] == expert_range[None, :, None]).astype(jnp.float32),
        axis=2,
    )
    source_weights = jnp.repeat(
        local_table.reshape(row_count, block_len, EXPERTS).transpose(0, 2, 1), group_len, axis=1
    )
    moe_sum = jnp.sum(source_weights[:, :, :, None] * back[:, :, :block_len], axis=1)
    grad_sum = jnp.sum(back[:, :, block_len:], axis=1)
    layer_out = (mixed_act.astype(jnp.float32) + moe_sum.reshape(tok_col, -1)).astype(jnp.bfloat16)
    mixed_grad = (out_grad.astype(jnp.float32) + grad_sum.reshape(tok_col, -1)).astype(jnp.bfloat16)
    expert_in_grad = lax.psum_scatter(
        grad_in.astype(jnp.bfloat16).astype(jnp.float32), "row", scatter_dimension=0, tiled=True
    ).astype(jnp.bfloat16)
    expert_out_grad = lax.psum_scatter(
        grad_out.astype(jnp.bfloat16).astype(jnp.float32), "row", scatter_dimension=1, tiled=True
    ).astype(jnp.bfloat16)
    cot_panel = gather_rows(mixed_grad, "col")
    hgrad_terms = jnp.dot(cot_panel, w_down.T, preferred_element_type=jnp.float32)
    down_grad = jnp.dot(hidden_full.T, cot_panel, preferred_element_type=jnp.float32).astype(
        jnp.bfloat16
    )
    hidden_grad = scatter_sum(hgrad_terms, "row")
    dpre_full = gather_rows((hidden_grad * gelu_slope(preact)).astype(jnp.bfloat16), "row")
    up_grad = jnp.dot(tok_panel.T, dpre_full, preferred_element_type=jnp.float32).astype(
        jnp.bfloat16
    )
    rows_in = dpre_full
    input_term = scatter_sum(jnp.dot(rows_in, w_up.T, preferred_element_type=jnp.float32), "col")
    tokens_grad = (mixed_grad.astype(jnp.float32) + input_term).astype(jnp.bfloat16)
    return (layer_out, tokens_grad, up_grad, down_grad, expert_in_grad, expert_out_grad)


def solution(mesh):
    in_specs = (
        P("col", "row"),
        P("row", "col"),
        P("col", "row"),
        P(None, "col"),
        P("col", None),
        P("col", None),
        P("col", None),
        P("col", "row"),
    )
    out_specs = (
        P("col", "row"),
        P("col", "row"),
        P("row", "col"),
        P("col", "row"),
        P("row", "col"),
        P("col", "row"),
    )
    return jax.shard_map(
        on_device, mesh=mesh, in_specs=in_specs, out_specs=out_specs, check_vma=False
    )
```

```python
import jax
import jax.numpy as jnp
from jax import lax
from jax.sharding import PartitionSpec as P

EXPERTS = 4


gelu_scale = 0.7978845608028654
gelu_cubic = 0.044715


def gelu_tanh(value):
    return 0.5 * value * (1.0 + jnp.tanh(gelu_scale * (value + gelu_cubic * value * value * value)))


def gelu_slope(value):
    inner = jnp.tanh(gelu_scale * (value + gelu_cubic * value * value * value))
    return 0.5 * (1.0 + inner) + 0.5 * value * (1.0 - inner * inner) * gelu_scale * (
        1.0 + 3.0 * gelu_cubic * value * value
    )


def slot_ranks(pairs):
    count = pairs.shape[-1]
    positions = jnp.arange(count, dtype=jnp.int32)
    earlier = positions[:, None] > positions[None, :]
    matching = pairs[..., :, None] == pairs[..., None, :]
    return jnp.sum((matching & earlier).astype(jnp.int32), axis=-1)


def gather_rows(part, axis_name):
    count = lax.axis_size(axis_name)
    spread = jnp.broadcast_to(part[None], (count,) + part.shape)
    got = lax.all_to_all(spread, axis_name, 0, 0, tiled=True)
    return got.reshape((count * part.shape[0],) + part.shape[1:])


def scatter_sum(terms, axis_name):
    count = lax.axis_size(axis_name)
    blocks = terms.astype(jnp.bfloat16).reshape((count, terms.shape[0] // count) + terms.shape[1:])
    got = lax.all_to_all(blocks, axis_name, 0, 0, tiled=True)
    return got.astype(jnp.float32).sum(axis=0)


def scatter_sum_cols(terms, axis_name):
    count = lax.axis_size(axis_name)
    got = lax.all_to_all(terms.astype(jnp.bfloat16), axis_name, 1, 0, tiled=True)
    return got.reshape((count, terms.shape[0], terms.shape[1] // count)).astype(jnp.float32).sum(axis=0)


def dense_exchange(payload, axis_name):
    shape = payload.shape
    flat = payload.reshape(shape[0], -1, 128)
    got = lax.all_to_all(flat, axis_name, 0, 0, tiled=True)
    return got.reshape(shape)


def swap_blocks(pair, count):
    arrays, tok, width = pair.shape
    block = tok // count
    parts = pair.reshape(arrays, count, block, width).transpose(1, 0, 2, 3)
    got = lax.all_to_all(parts.reshape(count, arrays * block, width), "row", 0, 0, tiled=True)
    got = got.reshape(count, arrays, block, width).transpose(1, 2, 0, 3)
    return got.reshape(arrays, block, count * width)


def unswap_blocks(pair, count):
    arrays, block, full = pair.shape
    width = full // count
    parts = pair.reshape(arrays, block, count, width).transpose(2, 0, 1, 3)
    got = lax.all_to_all(parts.reshape(count, arrays * block, width), "row", 0, 0, tiled=True)
    got = got.reshape(count, arrays, block, width).transpose(1, 0, 2, 3)
    return got.reshape(arrays, count * block, width)


def on_device(tokens, w_up, w_down, expert_in, expert_out, expert_ids, route_weights, out_grad):
    row_count = lax.axis_size("row")
    col_count = lax.axis_size("col")
    tok_col = tokens.shape[0]
    block_len = tok_col // row_count
    group_len = col_count // EXPERTS
    slot_cap = max(2, 3 * block_len // 4)
    model_width = expert_out.shape[1]
    my_row = lax.axis_index("row")
    own_grad = swap_blocks(out_grad[None], row_count)[0]
    ids_own = lax.dynamic_slice_in_dim(expert_ids, my_row * block_len, block_len, 0)
    weights_own = lax.dynamic_slice_in_dim(route_weights, my_row * block_len, block_len, 0)
    expert_range = jnp.arange(EXPERTS, dtype=jnp.int32)
    weight_table = jnp.sum(
        weights_own.astype(jnp.float32)[None, :, :]
        * (ids_own[None, :, :] == expert_range[:, None, None]).astype(jnp.float32),
        axis=2,
    )
    table_row = jnp.pad(
        weight_table.reshape(1, EXPERTS * block_len).astype(jnp.bfloat16),
        ((0, 0), (0, model_width - EXPERTS * block_len)),
    )
    grad_pack = jnp.concatenate([own_grad, table_row], axis=0)
    tokens_ready, grad_pack = lax.optimization_barrier((tokens, grad_pack))
    tok_panel = gather_rows(tokens_ready, "col")
    pack_all = lax.all_gather(grad_pack, "col", axis=0, tiled=False)
    my_expert = lax.axis_index("col") // group_len
    weights_recv = lax.dynamic_slice_in_dim(
        pack_all[:, block_len, : EXPERTS * block_len], my_expert * block_len, block_len, 1
    )
    grad_rows_in = (
        weights_recv.astype(jnp.float32)[:, :, None] * pack_all[:, :block_len].astype(jnp.float32)
    ).astype(jnp.bfloat16)
    up_terms = jnp.dot(tok_panel, w_up, preferred_element_type=jnp.float32)
    preact = scatter_sum(up_terms, "row")
    hidden_full = gather_rows(gelu_tanh(preact).astype(jnp.bfloat16), "row")
    rows_in = hidden_full
    down_terms, pack_all = lax.optimization_barrier(
        (jnp.dot(rows_in, w_down, preferred_element_type=jnp.float32), pack_all)
    )
    dense_term = scatter_sum(down_terms, "col")
    mixed_act = (tokens.astype(jnp.float32) + dense_term).astype(jnp.bfloat16)
    own_rows = swap_blocks(mixed_act[None], row_count)[0]
    scaled_flat = grad_rows_in.reshape(col_count * block_len, model_width)
    payload = jnp.broadcast_to(own_rows[None], (col_count,) + own_rows.shape)
    got = lax.all_to_all(payload, "col", 0, 0, tiled=True)
    got_flat = got.reshape(col_count * block_len, model_width)
    hid_units = expert_in.shape[1]
    e_pre = jnp.dot(got_flat, expert_in, preferred_element_type=jnp.float32).reshape(
        col_count, block_len, hid_units
    )
    g_dot = jnp.dot(scaled_flat, expert_out.T, preferred_element_type=jnp.float32).reshape(
        col_count, block_len, hid_units
    )
    e_hidden = gelu_tanh(e_pre).astype(jnp.bfloat16)
    e_dpre = (g_dot * gelu_slope(e_pre)).astype(jnp.bfloat16)
    blank = jnp.zeros_like(e_hidden)

    def at_rows(value, first):
        halves = [value, blank] if first else [blank, value]
        return jnp.concatenate(halves, axis=1).reshape(col_count * 2 * block_len, hid_units)

    back_flat = jnp.dot(
        at_rows(e_hidden, True), expert_out, preferred_element_type=jnp.float32
    ) + jnp.dot(at_rows(e_dpre, False), expert_in.T, preferred_element_type=jnp.float32)
    grad_in = jnp.dot(
        got_flat.T, e_dpre.reshape(col_count * block_len, hid_units), preferred_element_type=jnp.float32
    )
    grad_out = jnp.dot(
        e_hidden.reshape(col_count * block_len, hid_units).T, scaled_flat, preferred_element_type=jnp.float32
    )
    back = lax.all_to_all(
        back_flat.astype(jnp.bfloat16)
        .reshape(col_count, 2 * block_len, row_count, model_width // row_count)
        .transpose(2, 0, 1, 3)
        .reshape(row_count * col_count, 2 * block_len, model_width // row_count),
        ("row", "col"),
        0,
        0,
        tiled=True,
    ).astype(jnp.float32).reshape(row_count, col_count, 2 * block_len, model_width // row_count)
    local_table = jnp.sum(
        route_weights.astype(jnp.float32)[:, None, :]
        * (expert_ids[:, None, :] == expert_range[None, :, None]).astype(jnp.float32),
        axis=2,
    )
    source_weights = jnp.repeat(
        local_table.reshape(row_count, block_len, EXPERTS).transpose(0, 2, 1), group_len, axis=1
    )
    moe_sum = jnp.sum(source_weights[:, :, :, None] * back[:, :, :block_len], axis=1)
    grad_sum = jnp.sum(back[:, :, block_len:], axis=1)
    layer_out = (mixed_act.astype(jnp.float32) + moe_sum.reshape(tok_col, -1)).astype(jnp.bfloat16)
    mixed_grad = (out_grad.astype(jnp.float32) + grad_sum.reshape(tok_col, -1)).astype(jnp.bfloat16)
    expert_in_grad = lax.psum_scatter(
        grad_in.astype(jnp.bfloat16).astype(jnp.float32), "row", scatter_dimension=0, tiled=True
    ).astype(jnp.bfloat16)
    expert_out_grad = lax.psum_scatter(
        grad_out.astype(jnp.bfloat16).astype(jnp.float32), "row", scatter_dimension=1, tiled=True
    ).astype(jnp.bfloat16)
    cot_panel = gather_rows(mixed_grad, "col")
    hgrad_terms = jnp.dot(cot_panel, w_down.T, preferred_element_type=jnp.float32)
    down_grad = jnp.dot(hidden_full.T, cot_panel, preferred_element_type=jnp.float32).astype(
        jnp.bfloat16
    )
    hidden_grad = scatter_sum(hgrad_terms, "row")
    dpre_full = gather_rows((hidden_grad * gelu_slope(preact)).astype(jnp.bfloat16), "row")
    up_grad = jnp.dot(tok_panel.T, dpre_full, preferred_element_type=jnp.float32).astype(
        jnp.bfloat16
    )
    rows_in = dpre_full
    input_term = scatter_sum(jnp.dot(rows_in, w_up.T, preferred_element_type=jnp.float32), "col")
    tokens_grad = (mixed_grad.astype(jnp.float32) + input_term).astype(jnp.bfloat16)
    return (layer_out, tokens_grad, up_grad, down_grad, expert_in_grad, expert_out_grad)


def solution(mesh):
    in_specs = (
        P("col", "row"),
        P("row", "col"),
        P("col", "row"),
        P(None, "col"),
        P("col", None),
        P("col", None),
        P("col", None),
        P("col", "row"),
    )
    out_specs = (
        P("col", "row"),
        P("col", "row"),
        P("row", "col"),
        P("col", "row"),
        P("row", "col"),
        P("col", "row"),
    )
    return jax.shard_map(
        on_device, mesh=mesh, in_specs=in_specs, out_specs=out_specs, check_vma=False
    )
```

```python
import jax
import jax.numpy as jnp
from jax import lax
from jax.sharding import PartitionSpec as P

EXPERTS = 4


gelu_scale = 0.7978845608028654
gelu_cubic = 0.044715


def gelu_tanh(value):
    return 0.5 * value * (1.0 + jnp.tanh(gelu_scale * (value + gelu_cubic * value * value * value)))


def gelu_slope(value):
    inner = jnp.tanh(gelu_scale * (value + gelu_cubic * value * value * value))
    return 0.5 * (1.0 + inner) + 0.5 * value * (1.0 - inner * inner) * gelu_scale * (
        1.0 + 3.0 * gelu_cubic * value * value
    )


def slot_ranks(pairs):
    count = pairs.shape[-1]
    positions = jnp.arange(count, dtype=jnp.int32)
    earlier = positions[:, None] > positions[None, :]
    matching = pairs[..., :, None] == pairs[..., None, :]
    return jnp.sum((matching & earlier).astype(jnp.int32), axis=-1)


def gather_rows(part, axis_name):
    count = lax.axis_size(axis_name)
    spread = jnp.broadcast_to(part[None], (count,) + part.shape)
    got = lax.all_to_all(spread, axis_name, 0, 0, tiled=True)
    return got.reshape((count * part.shape[0],) + part.shape[1:])


def scatter_sum(terms, axis_name):
    count = lax.axis_size(axis_name)
    blocks = terms.astype(jnp.bfloat16).reshape((count, terms.shape[0] // count) + terms.shape[1:])
    got = lax.all_to_all(blocks, axis_name, 0, 0, tiled=True)
    return got.astype(jnp.float32).sum(axis=0)


def scatter_sum_cols(terms, axis_name):
    count = lax.axis_size(axis_name)
    got = lax.all_to_all(terms.astype(jnp.bfloat16), axis_name, 1, 0, tiled=True)
    return got.reshape((count, terms.shape[0], terms.shape[1] // count)).astype(jnp.float32).sum(axis=0)


def dense_exchange(payload, axis_name):
    shape = payload.shape
    flat = payload.reshape(shape[0], -1, 128)
    got = lax.all_to_all(flat, axis_name, 0, 0, tiled=True)
    return got.reshape(shape)


def swap_blocks(pair, count):
    arrays, tok, width = pair.shape
    block = tok // count
    parts = pair.reshape(arrays, count, block, width).transpose(1, 0, 2, 3)
    got = lax.all_to_all(parts.reshape(count, arrays * block, width), "row", 0, 0, tiled=True)
    got = got.reshape(count, arrays, block, width).transpose(1, 2, 0, 3)
    return got.reshape(arrays, block, count * width)


def unswap_blocks(pair, count):
    arrays, block, full = pair.shape
    width = full // count
    parts = pair.reshape(arrays, block, count, width).transpose(2, 0, 1, 3)
    got = lax.all_to_all(parts.reshape(count, arrays * block, width), "row", 0, 0, tiled=True)
    got = got.reshape(count, arrays, block, width).transpose(1, 0, 2, 3)
    return got.reshape(arrays, count * block, width)


def on_device(tokens, w_up, w_down, expert_in, expert_out, expert_ids, route_weights, out_grad):
    row_count = lax.axis_size("row")
    col_count = lax.axis_size("col")
    tok_col = tokens.shape[0]
    block_len = tok_col // row_count
    group_len = col_count // EXPERTS
    slot_cap = max(2, 3 * block_len // 4)
    model_width = expert_out.shape[1]
    my_row = lax.axis_index("row")
    own_grad = swap_blocks(out_grad[None], row_count)[0]
    ids_own = lax.dynamic_slice_in_dim(expert_ids, my_row * block_len, block_len, 0)
    weights_own = lax.dynamic_slice_in_dim(route_weights, my_row * block_len, block_len, 0)
    expert_range = jnp.arange(EXPERTS, dtype=jnp.int32)
    weight_table = jnp.sum(
        weights_own.astype(jnp.float32)[None, :, :]
        * (ids_own[None, :, :] == expert_range[:, None, None]).astype(jnp.float32),
        axis=2,
    )
    table_row = jnp.pad(
        weight_table.reshape(1, EXPERTS * block_len).astype(jnp.bfloat16),
        ((0, 0), (0, model_width - EXPERTS * block_len)),
    )
    grad_pack = jnp.concatenate([own_grad, table_row], axis=0)
    tokens_ready, grad_pack = lax.optimization_barrier((tokens, grad_pack))
    tok_panel = gather_rows(tokens_ready, "col")
    pack_all = lax.all_gather(grad_pack, "col", axis=0, tiled=False)
    my_expert = lax.axis_index("col") // group_len
    weights_recv = lax.dynamic_slice_in_dim(
        pack_all[:, block_len, : EXPERTS * block_len], my_expert * block_len, block_len, 1
    )
    grad_rows_in = (
        weights_recv.astype(jnp.float32)[:, :, None] * pack_all[:, :block_len].astype(jnp.float32)
    ).astype(jnp.bfloat16)
    up_terms = jnp.dot(tok_panel, w_up, preferred_element_type=jnp.float32)
    preact = scatter_sum(up_terms, "row")
    hidden_full = gather_rows(gelu_tanh(preact).astype(jnp.bfloat16), "row")
    rows_in = hidden_full
    dense_term = scatter_sum(jnp.dot(rows_in, w_down, preferred_element_type=jnp.float32), "col")
    dense_term, pack_all = lax.optimization_barrier((dense_term, pack_all))
    mixed_act = (tokens.astype(jnp.float32) + dense_term).astype(jnp.bfloat16)
    own_rows = swap_blocks(mixed_act[None], row_count)[0]
    scaled_flat = grad_rows_in.reshape(col_count * block_len, model_width)
    payload = jnp.broadcast_to(own_rows[None], (col_count,) + own_rows.shape)
    got = lax.all_to_all(payload, "col", 0, 0, tiled=True)
    got_flat = got.reshape(col_count * block_len, model_width)
    hid_units = expert_in.shape[1]
    e_pre = jnp.dot(got_flat, expert_in, preferred_element_type=jnp.float32).reshape(
        col_count, block_len, hid_units
    )
    g_dot = jnp.dot(scaled_flat, expert_out.T, preferred_element_type=jnp.float32).reshape(
        col_count, block_len, hid_units
    )
    e_hidden = gelu_tanh(e_pre).astype(jnp.bfloat16)
    e_dpre = (g_dot * gelu_slope(e_pre)).astype(jnp.bfloat16)
    blank = jnp.zeros_like(e_hidden)

    def at_rows(value, first):
        halves = [value, blank] if first else [blank, value]
        return jnp.concatenate(halves, axis=1).reshape(col_count * 2 * block_len, hid_units)

    back_flat = jnp.dot(
        at_rows(e_hidden, True), expert_out, preferred_element_type=jnp.float32
    ) + jnp.dot(at_rows(e_dpre, False), expert_in.T, preferred_element_type=jnp.float32)
    grad_in = jnp.dot(
        got_flat.T, e_dpre.reshape(col_count * block_len, hid_units), preferred_element_type=jnp.float32
    )
    grad_out = jnp.dot(
        e_hidden.reshape(col_count * block_len, hid_units).T, scaled_flat, preferred_element_type=jnp.float32
    )
    back = lax.all_to_all(
        back_flat.astype(jnp.bfloat16)
        .reshape(col_count, 2 * block_len, row_count, model_width // row_count)
        .transpose(2, 0, 1, 3)
        .reshape(row_count * col_count, 2 * block_len, model_width // row_count),
        ("row", "col"),
        0,
        0,
        tiled=True,
    ).astype(jnp.float32).reshape(row_count, col_count, 2 * block_len, model_width // row_count)
    local_table = jnp.sum(
        route_weights.astype(jnp.float32)[:, None, :]
        * (expert_ids[:, None, :] == expert_range[None, :, None]).astype(jnp.float32),
        axis=2,
    )
    source_weights = jnp.repeat(
        local_table.reshape(row_count, block_len, EXPERTS).transpose(0, 2, 1), group_len, axis=1
    )
    moe_sum = jnp.sum(source_weights[:, :, :, None] * back[:, :, :block_len], axis=1)
    grad_sum = jnp.sum(back[:, :, block_len:], axis=1)
    layer_out = (mixed_act.astype(jnp.float32) + moe_sum.reshape(tok_col, -1)).astype(jnp.bfloat16)
    mixed_grad = (out_grad.astype(jnp.float32) + grad_sum.reshape(tok_col, -1)).astype(jnp.bfloat16)
    expert_in_grad = lax.psum_scatter(
        grad_in.astype(jnp.bfloat16).astype(jnp.float32), "row", scatter_dimension=0, tiled=True
    ).astype(jnp.bfloat16)
    expert_out_grad = lax.psum_scatter(
        grad_out.astype(jnp.bfloat16).astype(jnp.float32), "row", scatter_dimension=1, tiled=True
    ).astype(jnp.bfloat16)
    cot_panel = gather_rows(mixed_grad, "col")
    hgrad_terms = jnp.dot(cot_panel, w_down.T, preferred_element_type=jnp.float32)
    down_grad = jnp.dot(hidden_full.T, cot_panel, preferred_element_type=jnp.float32).astype(
        jnp.bfloat16
    )
    hidden_grad = scatter_sum(hgrad_terms, "row")
    dpre_full = gather_rows((hidden_grad * gelu_slope(preact)).astype(jnp.bfloat16), "row")
    up_grad = jnp.dot(tok_panel.T, dpre_full, preferred_element_type=jnp.float32).astype(
        jnp.bfloat16
    )
    rows_in = dpre_full
    input_term = scatter_sum(jnp.dot(rows_in, w_up.T, preferred_element_type=jnp.float32), "col")
    tokens_grad = (mixed_grad.astype(jnp.float32) + input_term).astype(jnp.bfloat16)
    return (layer_out, tokens_grad, up_grad, down_grad, expert_in_grad, expert_out_grad)


def solution(mesh):
    in_specs = (
        P("col", "row"),
        P("row", "col"),
        P("col", "row"),
        P(None, "col"),
        P("col", None),
        P("col", None),
        P("col", None),
        P("col", "row"),
    )
    out_specs = (
        P("col", "row"),
        P("col", "row"),
        P("row", "col"),
        P("col", "row"),
        P("row", "col"),
        P("col", "row"),
    )
    return jax.shard_map(
        on_device, mesh=mesh, in_specs=in_specs, out_specs=out_specs, check_vma=False
    )
```

```python
import jax
import jax.numpy as jnp
from jax import lax
from jax.sharding import PartitionSpec as P

EXPERTS = 4


gelu_scale = 0.7978845608028654
gelu_cubic = 0.044715


def gelu_tanh(value):
    return 0.5 * value * (1.0 + jnp.tanh(gelu_scale * (value + gelu_cubic * value * value * value)))


def gelu_slope(value):
    inner = jnp.tanh(gelu_scale * (value + gelu_cubic * value * value * value))
    return 0.5 * (1.0 + inner) + 0.5 * value * (1.0 - inner * inner) * gelu_scale * (
        1.0 + 3.0 * gelu_cubic * value * value
    )


def slot_ranks(pairs):
    count = pairs.shape[-1]
    positions = jnp.arange(count, dtype=jnp.int32)
    earlier = positions[:, None] > positions[None, :]
    matching = pairs[..., :, None] == pairs[..., None, :]
    return jnp.sum((matching & earlier).astype(jnp.int32), axis=-1)


def gather_rows(part, axis_name):
    count = lax.axis_size(axis_name)
    spread = jnp.broadcast_to(part[None], (count,) + part.shape)
    got = lax.all_to_all(spread, axis_name, 0, 0, tiled=True)
    return got.reshape((count * part.shape[0],) + part.shape[1:])


def scatter_sum(terms, axis_name):
    count = lax.axis_size(axis_name)
    blocks = terms.astype(jnp.bfloat16).reshape((count, terms.shape[0] // count) + terms.shape[1:])
    got = lax.all_to_all(blocks, axis_name, 0, 0, tiled=True)
    return got.astype(jnp.float32).sum(axis=0)


def scatter_sum_cols(terms, axis_name):
    count = lax.axis_size(axis_name)
    got = lax.all_to_all(terms.astype(jnp.bfloat16), axis_name, 1, 0, tiled=True)
    return got.reshape((count, terms.shape[0], terms.shape[1] // count)).astype(jnp.float32).sum(axis=0)


def dense_exchange(payload, axis_name):
    shape = payload.shape
    flat = payload.reshape(shape[0], -1, 128)
    got = lax.all_to_all(flat, axis_name, 0, 0, tiled=True)
    return got.reshape(shape)


def swap_blocks(pair, count):
    arrays, tok, width = pair.shape
    block = tok // count
    parts = pair.reshape(arrays, count, block, width).transpose(1, 0, 2, 3)
    got = lax.all_to_all(parts.reshape(count, arrays * block, width), "row", 0, 0, tiled=True)
    got = got.reshape(count, arrays, block, width).transpose(1, 2, 0, 3)
    return got.reshape(arrays, block, count * width)


def unswap_blocks(pair, count):
    arrays, block, full = pair.shape
    width = full // count
    parts = pair.reshape(arrays, block, count, width).transpose(2, 0, 1, 3)
    got = lax.all_to_all(parts.reshape(count, arrays * block, width), "row", 0, 0, tiled=True)
    got = got.reshape(count, arrays, block, width).transpose(1, 0, 2, 3)
    return got.reshape(arrays, count * block, width)


def on_device(tokens, w_up, w_down, expert_in, expert_out, expert_ids, route_weights, out_grad):
    row_count = lax.axis_size("row")
    col_count = lax.axis_size("col")
    tok_col = tokens.shape[0]
    block_len = tok_col // row_count
    group_len = col_count // EXPERTS
    slot_cap = max(2, 3 * block_len // 4)
    model_width = expert_out.shape[1]
    my_row = lax.axis_index("row")
    own_grad = swap_blocks(out_grad[None], row_count)[0]
    ids_own = lax.dynamic_slice_in_dim(expert_ids, my_row * block_len, block_len, 0)
    weights_own = lax.dynamic_slice_in_dim(route_weights, my_row * block_len, block_len, 0)
    expert_range = jnp.arange(EXPERTS, dtype=jnp.int32)
    weight_table = jnp.sum(
        weights_own.astype(jnp.float32)[None, :, :]
        * (ids_own[None, :, :] == expert_range[:, None, None]).astype(jnp.float32),
        axis=2,
    )
    table_row = jnp.pad(
        weight_table.reshape(1, EXPERTS * block_len).astype(jnp.bfloat16),
        ((0, 0), (0, model_width - EXPERTS * block_len)),
    )
    grad_pack = jnp.concatenate([own_grad, table_row], axis=0)
    tokens_ready, grad_pack = lax.optimization_barrier((tokens, grad_pack))
    tok_panel = gather_rows(tokens_ready, "col")
    pack_all = lax.all_gather(grad_pack, "col", axis=0, tiled=False)
    my_expert = lax.axis_index("col") // group_len
    weights_recv = lax.dynamic_slice_in_dim(
        pack_all[:, block_len, : EXPERTS * block_len], my_expert * block_len, block_len, 1
    )
    grad_rows_in = (
        weights_recv.astype(jnp.float32)[:, :, None] * pack_all[:, :block_len].astype(jnp.float32)
    ).astype(jnp.bfloat16)
    up_terms = jnp.dot(tok_panel, w_up, preferred_element_type=jnp.float32)
    preact = scatter_sum(up_terms, "row")
    hidden_full = gather_rows(gelu_tanh(preact).astype(jnp.bfloat16), "row")
    rows_in = hidden_full
    down_terms, pack_all = lax.optimization_barrier(
        (jnp.dot(rows_in, w_down, preferred_element_type=jnp.float32), pack_all)
    )
    dense_term = scatter_sum(down_terms, "col")
    mixed_act = (tokens.astype(jnp.float32) + dense_term).astype(jnp.bfloat16)
    own_rows = swap_blocks(mixed_act[None], row_count)[0]
    scaled_flat = grad_rows_in.reshape(col_count * block_len, model_width)
    payload = jnp.broadcast_to(own_rows[None], (col_count,) + own_rows.shape)
    got = lax.all_to_all(payload, "col", 0, 0, tiled=True)
    got_flat = got.reshape(col_count * block_len, model_width)
    hid_units = expert_in.shape[1]
    e_pre = jnp.dot(got_flat, expert_in, preferred_element_type=jnp.float32).reshape(
        col_count, block_len, hid_units
    )
    g_dot = jnp.dot(scaled_flat, expert_out.T, preferred_element_type=jnp.float32).reshape(
        col_count, block_len, hid_units
    )
    e_hidden = gelu_tanh(e_pre).astype(jnp.bfloat16)
    e_dpre = (g_dot * gelu_slope(e_pre)).astype(jnp.bfloat16)
    blank = jnp.zeros_like(e_hidden)

    def at_rows(value, first):
        halves = [value, blank] if first else [blank, value]
        return jnp.concatenate(halves, axis=1).reshape(col_count * 2 * block_len, hid_units)

    back_flat = jnp.dot(
        at_rows(e_hidden, True), expert_out, preferred_element_type=jnp.float32
    ) + jnp.dot(at_rows(e_dpre, False), expert_in.T, preferred_element_type=jnp.float32)
    grad_in = jnp.dot(
        got_flat.T, e_dpre.reshape(col_count * block_len, hid_units), preferred_element_type=jnp.float32
    )
    grad_out = jnp.dot(
        e_hidden.reshape(col_count * block_len, hid_units).T, scaled_flat, preferred_element_type=jnp.float32
    )
    back = lax.all_to_all(
        back_flat.astype(jnp.bfloat16).reshape(col_count, 2 * block_len, model_width),
        "col",
        0,
        0,
        tiled=True,
    ).astype(jnp.float32)
    source_weights = jnp.repeat(weight_table, group_len, axis=0)
    moe_sum = jnp.sum(source_weights[:, :, None] * back[:, :block_len], axis=0)
    grad_sum = jnp.sum(back[:, block_len:], axis=0)
    layer_rows = (own_rows.astype(jnp.float32) + moe_sum).astype(jnp.bfloat16)
    grad_rows = (own_grad.astype(jnp.float32) + grad_sum).astype(jnp.bfloat16)
    out_both = unswap_blocks(jnp.stack([layer_rows, grad_rows]), row_count)
    layer_out, mixed_grad = out_both[0], out_both[1]
    expert_in_grad = lax.psum_scatter(
        grad_in.astype(jnp.bfloat16).astype(jnp.float32), "row", scatter_dimension=0, tiled=True
    ).astype(jnp.bfloat16)
    expert_out_grad = lax.psum_scatter(
        grad_out.astype(jnp.bfloat16).astype(jnp.float32), "row", scatter_dimension=1, tiled=True
    ).astype(jnp.bfloat16)
    cot_panel = gather_rows(mixed_grad, "col")
    hgrad_terms = jnp.dot(cot_panel, w_down.T, preferred_element_type=jnp.float32)
    down_grad = jnp.dot(hidden_full.T, cot_panel, preferred_element_type=jnp.float32).astype(
        jnp.bfloat16
    )
    hidden_grad = scatter_sum(hgrad_terms, "row")
    dpre_full = gather_rows((hidden_grad * gelu_slope(preact)).astype(jnp.bfloat16), "row")
    up_grad = jnp.dot(tok_panel.T, dpre_full, preferred_element_type=jnp.float32).astype(
        jnp.bfloat16
    )
    rows_in = dpre_full
    input_term = scatter_sum(jnp.dot(rows_in, w_up.T, preferred_element_type=jnp.float32), "col")
    tokens_grad = (mixed_grad.astype(jnp.float32) + input_term).astype(jnp.bfloat16)
    return (layer_out, tokens_grad, up_grad, down_grad, expert_in_grad, expert_out_grad)


def solution(mesh):
    in_specs = (
        P("col", "row"),
        P("row", "col"),
        P("col", "row"),
        P(None, "col"),
        P("col", None),
        P("col", None),
        P("col", None),
        P("col", "row"),
    )
    out_specs = (
        P("col", "row"),
        P("col", "row"),
        P("row", "col"),
        P("col", "row"),
        P("row", "col"),
        P("col", "row"),
    )
    return jax.shard_map(
        on_device, mesh=mesh, in_specs=in_specs, out_specs=out_specs, check_vma=False
    )
```

```python
import jax
import jax.numpy as jnp
from jax import lax
from jax.sharding import PartitionSpec as P

EXPERTS = 4


gelu_scale = 0.7978845608028654
gelu_cubic = 0.044715


def gelu_tanh(value):
    return 0.5 * value * (1.0 + jnp.tanh(gelu_scale * (value + gelu_cubic * value * value * value)))


def gelu_slope(value):
    inner = jnp.tanh(gelu_scale * (value + gelu_cubic * value * value * value))
    return 0.5 * (1.0 + inner) + 0.5 * value * (1.0 - inner * inner) * gelu_scale * (
        1.0 + 3.0 * gelu_cubic * value * value
    )


def slot_ranks(pairs):
    count = pairs.shape[-1]
    positions = jnp.arange(count, dtype=jnp.int32)
    earlier = positions[:, None] > positions[None, :]
    matching = pairs[..., :, None] == pairs[..., None, :]
    return jnp.sum((matching & earlier).astype(jnp.int32), axis=-1)


def gather_rows(part, axis_name):
    count = lax.axis_size(axis_name)
    spread = jnp.broadcast_to(part[None], (count,) + part.shape)
    got = lax.all_to_all(spread, axis_name, 0, 0, tiled=True)
    return got.reshape((count * part.shape[0],) + part.shape[1:])


def scatter_sum(terms, axis_name):
    count = lax.axis_size(axis_name)
    blocks = terms.astype(jnp.bfloat16).reshape((count, terms.shape[0] // count) + terms.shape[1:])
    got = lax.all_to_all(blocks, axis_name, 0, 0, tiled=True)
    return got.astype(jnp.float32).sum(axis=0)


def scatter_sum_cols(terms, axis_name):
    count = lax.axis_size(axis_name)
    got = lax.all_to_all(terms.astype(jnp.bfloat16), axis_name, 1, 0, tiled=True)
    return got.reshape((count, terms.shape[0], terms.shape[1] // count)).astype(jnp.float32).sum(axis=0)


def dense_exchange(payload, axis_name):
    shape = payload.shape
    flat = payload.reshape(shape[0], -1, 128)
    got = lax.all_to_all(flat, axis_name, 0, 0, tiled=True)
    return got.reshape(shape)


def swap_blocks(pair, count):
    arrays, tok, width = pair.shape
    block = tok // count
    parts = pair.reshape(arrays, count, block, width).transpose(1, 0, 2, 3)
    got = lax.all_to_all(parts.reshape(count, arrays * block, width), "row", 0, 0, tiled=True)
    got = got.reshape(count, arrays, block, width).transpose(1, 2, 0, 3)
    return got.reshape(arrays, block, count * width)


def unswap_blocks(pair, count):
    arrays, block, full = pair.shape
    width = full // count
    parts = pair.reshape(arrays, block, count, width).transpose(2, 0, 1, 3)
    got = lax.all_to_all(parts.reshape(count, arrays * block, width), "row", 0, 0, tiled=True)
    got = got.reshape(count, arrays, block, width).transpose(1, 0, 2, 3)
    return got.reshape(arrays, count * block, width)


def on_device(tokens, w_up, w_down, expert_in, expert_out, expert_ids, route_weights, out_grad):
    row_count = lax.axis_size("row")
    col_count = lax.axis_size("col")
    tok_col = tokens.shape[0]
    block_len = tok_col // row_count
    group_len = col_count // EXPERTS
    slot_cap = max(2, 3 * block_len // 4)
    model_width = expert_out.shape[1]
    my_row = lax.axis_index("row")
    own_grad = swap_blocks(out_grad[None], row_count)[0]
    ids_own = lax.dynamic_slice_in_dim(expert_ids, my_row * block_len, block_len, 0)
    weights_own = lax.dynamic_slice_in_dim(route_weights, my_row * block_len, block_len, 0)
    expert_range = jnp.arange(EXPERTS, dtype=jnp.int32)
    weight_table = jnp.sum(
        weights_own.astype(jnp.float32)[None, :, :]
        * (ids_own[None, :, :] == expert_range[:, None, None]).astype(jnp.float32),
        axis=2,
    )
    table_row = jnp.pad(
        weight_table.reshape(1, EXPERTS * block_len).astype(jnp.bfloat16),
        ((0, 0), (0, model_width - EXPERTS * block_len)),
    )
    grad_pack = jnp.concatenate([own_grad, table_row], axis=0)
    tokens_ready, grad_pack = lax.optimization_barrier((tokens, grad_pack))
    tok_panel = gather_rows(tokens_ready, "col")
    pack_all = lax.all_gather(grad_pack, "col", axis=0, tiled=False)
    my_expert = lax.axis_index("col") // group_len
    weights_recv = lax.dynamic_slice_in_dim(
        pack_all[:, block_len, : EXPERTS * block_len], my_expert * block_len, block_len, 1
    )
    grad_rows_in = (
        weights_recv.astype(jnp.float32)[:, :, None] * pack_all[:, :block_len].astype(jnp.float32)
    ).astype(jnp.bfloat16)
    up_terms = jnp.dot(tok_panel, w_up, preferred_element_type=jnp.float32)
    preact = scatter_sum(up_terms, "row")
    hidden_full = gather_rows(gelu_tanh(preact).astype(jnp.bfloat16), "row")
    rows_in = hidden_full
    down_terms, pack_all = lax.optimization_barrier(
        (jnp.dot(rows_in, w_down, preferred_element_type=jnp.float32), pack_all)
    )
    dense_term = scatter_sum(down_terms, "col")
    mixed_act = (tokens.astype(jnp.float32) + dense_term).astype(jnp.bfloat16)
    own_rows = swap_blocks(mixed_act[None], row_count)[0]
    scaled_flat = grad_rows_in.reshape(col_count * block_len, model_width)
    payload = jnp.broadcast_to(own_rows[None], (col_count,) + own_rows.shape)
    got = lax.all_to_all(payload, "col", 0, 0, tiled=True)
    got_flat = got.reshape(col_count * block_len, model_width)
    hid_units = expert_in.shape[1]
    e_pre = jnp.dot(got_flat, expert_in, preferred_element_type=jnp.float32).reshape(
        col_count, block_len, hid_units
    )
    g_dot = jnp.dot(scaled_flat, expert_out.T, preferred_element_type=jnp.float32).reshape(
        col_count, block_len, hid_units
    )
    e_hidden = gelu_tanh(e_pre).astype(jnp.bfloat16)
    e_dpre = (g_dot * gelu_slope(e_pre)).astype(jnp.bfloat16)
    blank = jnp.zeros_like(e_hidden)

    def at_rows(value, first):
        halves = [value, blank] if first else [blank, value]
        return jnp.concatenate(halves, axis=1).reshape(col_count * 2 * block_len, hid_units)

    back_flat = jnp.dot(
        at_rows(e_hidden, True), expert_out, preferred_element_type=jnp.float32
    ) + jnp.dot(at_rows(e_dpre, False), expert_in.T, preferred_element_type=jnp.float32)
    grad_in = jnp.dot(
        got_flat.T, e_dpre.reshape(col_count * block_len, hid_units), preferred_element_type=jnp.float32
    )
    grad_out = jnp.dot(
        e_hidden.reshape(col_count * block_len, hid_units).T, scaled_flat, preferred_element_type=jnp.float32
    )
    back = lax.all_to_all(
        back_flat.astype(jnp.bfloat16)
        .reshape(col_count, 2 * block_len, row_count, model_width // row_count)
        .transpose(2, 0, 1, 3)
        .reshape(row_count * col_count, 2 * block_len, model_width // row_count),
        ("row", "col"),
        0,
        0,
        tiled=True,
    ).astype(jnp.float32).reshape(row_count, col_count, 2 * block_len, model_width // row_count)
    local_table = jnp.sum(
        route_weights.astype(jnp.float32)[:, None, :]
        * (expert_ids[:, None, :] == expert_range[None, :, None]).astype(jnp.float32),
        axis=2,
    )
    source_weights = jnp.repeat(
        local_table.reshape(row_count, block_len, EXPERTS).transpose(0, 2, 1), group_len, axis=1
    )
    moe_sum = jnp.sum(source_weights[:, :, :, None] * back[:, :, :block_len], axis=1)
    grad_sum = jnp.sum(back[:, :, block_len:], axis=1)
    layer_out = (mixed_act.astype(jnp.float32) + moe_sum.reshape(tok_col, -1)).astype(jnp.bfloat16)
    mixed_grad = (out_grad.astype(jnp.float32) + grad_sum.reshape(tok_col, -1)).astype(jnp.bfloat16)
    expert_in_grad = lax.psum_scatter(
        grad_in.astype(jnp.bfloat16), "row", scatter_dimension=0, tiled=True
    ).astype(jnp.bfloat16)
    expert_out_grad = lax.psum_scatter(
        grad_out.astype(jnp.bfloat16), "row", scatter_dimension=1, tiled=True
    ).astype(jnp.bfloat16)
    cot_panel = gather_rows(mixed_grad, "col")
    hgrad_terms = jnp.dot(cot_panel, w_down.T, preferred_element_type=jnp.float32)
    down_grad = jnp.dot(hidden_full.T, cot_panel, preferred_element_type=jnp.float32).astype(
        jnp.bfloat16
    )
    hidden_grad = scatter_sum(hgrad_terms, "row")
    dpre_full = gather_rows((hidden_grad * gelu_slope(preact)).astype(jnp.bfloat16), "row")
    up_grad = jnp.dot(tok_panel.T, dpre_full, preferred_element_type=jnp.float32).astype(
        jnp.bfloat16
    )
    rows_in = dpre_full
    input_term = scatter_sum(jnp.dot(rows_in, w_up.T, preferred_element_type=jnp.float32), "col")
    tokens_grad = (mixed_grad.astype(jnp.float32) + input_term).astype(jnp.bfloat16)
    return (layer_out, tokens_grad, up_grad, down_grad, expert_in_grad, expert_out_grad)


def solution(mesh):
    in_specs = (
        P("col", "row"),
        P("row", "col"),
        P("col", "row"),
        P(None, "col"),
        P("col", None),
        P("col", None),
        P("col", None),
        P("col", "row"),
    )
    out_specs = (
        P("col", "row"),
        P("col", "row"),
        P("row", "col"),
        P("col", "row"),
        P("row", "col"),
        P("col", "row"),
    )
    return jax.shard_map(
        on_device, mesh=mesh, in_specs=in_specs, out_specs=out_specs, check_vma=False
    )
```
